32 devices in a mesh: freq: 2 (over y), clus: 4 (over z), src: 2 (over x), sub: 2 (over core).
Axes of the slice: x: 2, y: 2, z: 4, core: 2. Of those that a mesh axis runs over, the one named last changes fastest.
Arguments:
- charges: bfloat16 [512, 48, 128], P(('freq', 'src'), 'clus'), parts along dimension 0, may hold values from -6 to 6
- geometry: float32 [4, 48, 256], replicated, may hold values from -4 to 4, as said below
- wavenumber: float32 [2], P('freq'), parts along dimension 0, may hold values from 0.3 to 2
- requests: int32 [8, 4, 4], P(('clus', 'sub')), may hold values from -1 to 11, as said below
- pairs: int32 [48, 2, 32], P('clus', 'sub'), may hold values from 0 to 15, as said below
- counts: int32 [48, 2], P('clus', 'sub'), may hold values from 1 to 32, as said below
Outputs:
- iterate: bfloat16 [512, 48, 128], P(('freq', 'src'), 'clus'), parts along dimension 0
- image: float32 [512, 48, 128], P(('freq', 'src', 'sub'), 'clus'), parts along dimension 0
The draws below stay inside these ranges and needn't reach their ends.
There are 2 independent parts, one for each index of `freq`. The reference program is written for one: setup_inputs(seed, part) draws one part's arguments, and reference() takes and returns one part's arrays. A program takes and returns all parts, laid end to end along the dimension named above; an argument that names none is the same for every part. Nothing has to cross between parts.
Inputs may be any that keep to these rules, and one draw needn't show every extreme that they name: `geometry`: rows: x and y, depth z from -1 to -0.05, panel area from 0.05 to 0.5. `requests`: each row's live entries are distinct cluster numbers and come first, -1 marks an empty slot; in every block the row of the block's own clus index holds 4 live entries. `pairs`: every entry d * 4 + k names a live entry requests[b, d, k] of the block b of the target cluster's owner and half. `counts`: 32 is reached in every draw.
All inputs are finite; a program needn't handle non-finite values.
Results may differ from the reference program's by a relative error of at most 0.0049.
Values may be sent and summed in bfloat16 or wider, within the bound.
No kernel may reach another device: no remote copies, remote signals or barrier semaphores. Data moves between devices by JAX's collectives and lax.ppermute only.
A program may use at most 64 MiB of HBM per device.

```python
import math
import jax
import jax.numpy as jnp
from jax import lax

CS = 256
RHS = 64
CPD = 12
CAP = 4
PPT = 32
CLUSTERS = 48
N_CLUS = 4
N_SUB = 2


def draw_geometry(key, part):
    subkeys = jax.random.split(key, 6)
    panel_shape = (CLUSTERS, CS)
    coord_x = jax.random.uniform(subkeys[0], panel_shape, minval=-4.0, maxval=4.0)
    coord_y = jax.random.uniform(subkeys[1], panel_shape, minval=-4.0, maxval=4.0)
    coord_z = jax.random.uniform(subkeys[4], panel_shape, minval=-1.0, maxval=-0.05)
    log_area = jax.random.uniform(subkeys[5], panel_shape, minval=jnp.log(0.05), maxval=jnp.log(0.5))
    panel_area = jnp.clip(jnp.exp(log_area), 0.05, 0.5)
    return jnp.stack([coord_x, coord_y, coord_z, panel_area]).astype(jnp.float32)


def request_table(key):
    subkeys = jax.random.split(key, 2)
    block_total = N_CLUS * N_SUB
    live_count = jax.random.randint(subkeys[0], (block_total, N_CLUS), 0, CAP + 1)
    owner = jnp.arange(block_total) // N_SUB
    live_count = jnp.where(jnp.arange(N_CLUS)[None, :] == owner[:, None], CAP, live_count)
    scores = jax.random.randint(subkeys[1], (block_total, N_CLUS, CPD), 0, 1 << 20) * CPD + jnp.arange(CPD)
    ordering = jnp.argsort(scores, axis=-1)[..., :CAP]
    return jnp.where(jnp.arange(CAP) < live_count[..., None], ordering, -1).astype(jnp.int32)


def draw_requests(key, part):
    return request_table(jax.random.fold_in(key, 7))


def draw_pairs(key, part):
    table = request_table(jax.random.fold_in(key, 7))
    block_total = N_CLUS * N_SUB
    is_live = (table.reshape(block_total, N_CLUS * CAP) >= 0).astype(jnp.int32)
    ordering = jnp.argsort(1 - is_live, axis=-1, stable=True)
    live_total = jnp.sum(is_live, axis=-1)
    owner_block = (jnp.arange(CLUSTERS) // CPD)[:, None] * N_SUB + jnp.arange(N_SUB)[None, :]
    raw_draws = jax.random.randint(jax.random.fold_in(key, 8), (CLUSTERS, N_SUB, PPT), 0, 1 << 20)
    pick_index = raw_draws % live_total[owner_block][..., None]
    return jnp.take_along_axis(ordering[owner_block], pick_index, axis=-1).astype(jnp.int32)


def draw_counts(key, part):
    subkeys = jax.random.split(key, 5)
    load_level = jax.random.randint(subkeys[0], (N_CLUS, N_SUB), PPT // 8, PPT // 2 + 1)
    full_block = jax.random.randint(subkeys[1], (N_CLUS, N_SUB), 0, 8) == 0
    forced = jax.random.randint(subkeys[2], (), 0, N_CLUS * N_SUB)
    block_grid = jnp.arange(N_CLUS * N_SUB).reshape(N_CLUS, N_SUB)
    load_level = jnp.where(full_block | (block_grid == forced), PPT, load_level)
    load_level = jnp.maximum(load_level, 1)
    drawn = jax.random.randint(subkeys[3], (N_CLUS, CPD, N_SUB), 1, load_level[:, None, :] + 1)
    chosen_target = jax.random.randint(subkeys[4], (N_CLUS, 1, N_SUB), 0, CPD)
    drawn = jnp.where(jnp.arange(CPD)[None, :, None] == chosen_target, load_level[:, None, :], drawn)
    return drawn.reshape(CLUSTERS, N_SUB).astype(jnp.int32)


def levels(own_key, shape, shards, low, top_value):
    def one(position, shards_of):
        draws = jax.random.uniform(jax.random.fold_in(jax.random.fold_in(own_key, 6), position), (shards_of,), jnp.float32, low / len(shards), top_value / len(shards))
        return jnp.repeat(jnp.exp(draws), shape[position] // shards_of).reshape((-1,) + (1,) * (len(shape) - position - 1))

    gain = one(*shards[0])
    for cut in shards[1:]:
        gain = gain * one(*cut)
    return gain


def gaussian(key, dims, width, limit, shards=(), kind=jnp.bfloat16):
    entries = jax.random.normal(key, dims, jnp.float32) * width
    if len(shards) > 0:
        entries = levels(key, dims, shards, -0.22, 0.18) * entries
    return jnp.clip(entries, min=-limit, max=limit).astype(kind)


def setup_inputs(seed: int = 0, part: int = 0) -> dict:
    key_of = jax.random.split(jax.random.key(seed), 7)
    own_keys = jax.random.split(jax.random.fold_in(key_of[6], part), 7)
    return {
        "charges": gaussian(own_keys[0], (CS, CLUSTERS, 2 * RHS), 1.0, 6.0, ((0, 2), (1, 4))),
        "geometry": draw_geometry(jax.random.fold_in(key_of[6], 71), part),
        "wavenumber": jnp.clip(jnp.exp(jax.random.uniform(own_keys[2], (1,), jnp.float32, math.log(0.3), math.log(2.0))), 0.3, 2.0),
        "requests": draw_requests(jax.random.fold_in(key_of[6], 71), part),
        "pairs": draw_pairs(jax.random.fold_in(key_of[6], 71), part),
        "counts": draw_counts(jax.random.fold_in(key_of[6], 71), part),
    }


quarter_turn = 0.7853981633974483
two_pi = 6.283185307179586
inverse_four_pi = 0.07957747154594767

def green_tiles(target_geo, source_geo, wavenum, weight):
    delta_x = target_geo[0][:, :, None] - source_geo[0][:, None, :]
    delta_y = target_geo[1][:, :, None] - source_geo[1][:, None, :]
    delta_z = target_geo[2][:, :, None] - source_geo[2][:, None, :]
    depth_sum = target_geo[2][:, :, None] + source_geo[2][:, None, :]
    panel_area = source_geo[3][:, None, :]
    planar = delta_x * delta_x + delta_y * delta_y
    direct = 1.0 / jnp.sqrt(planar + delta_z * delta_z + panel_area)
    mirror = 1.0 / jnp.sqrt(planar + depth_sum * depth_sum + panel_area)
    horizon = jnp.sqrt(planar)
    phase_angle = wavenum * horizon + quarter_turn
    amplitude = two_pi * wavenum * jnp.exp(wavenum * depth_sum) / jnp.sqrt(1.0 + wavenum * horizon)
    scaling = panel_area * inverse_four_pi * weight[:, None, :]
    real_part = (scaling * (direct + mirror - amplitude * jnp.sin(phase_angle))).astype(jnp.bfloat16)
    imag_part = (scaling * amplitude * jnp.cos(phase_angle)).astype(jnp.bfloat16)
    return (real_part, imag_part)

def apply_operator(values, geometry, wavenumber, requests, pairs, counts):
    wavenum = wavenumber[0]
    clusters_all = geometry.shape[1]
    halves = pairs.shape[1]
    owner = jnp.arange(clusters_all, dtype=jnp.int32) // CPD
    block_ids = owner[:, None] * halves + jnp.arange(halves, dtype=jnp.int32)[None, :]
    source_device = pairs // CAP
    source_slot = pairs % CAP
    local_cluster = requests[block_ids[:, :, None], source_device, source_slot]
    source_cluster = (source_device * CPD + local_cluster).astype(jnp.int32)
    is_live = (jnp.arange(PPT, dtype=jnp.int32)[None, None, :] < counts[:, :, None]).astype(jnp.float32)
    half_width = values.shape[2] // 2

    def one_cluster(target):
        cluster_ids = source_cluster[target].reshape(-1)
        weight = jnp.repeat(is_live[target].reshape(-1), CS)[None, :]
        target_geo = geometry[:, target][:, None, :]
        source_geo = jnp.take(geometry, cluster_ids, axis=1).reshape(4, 1, -1)
        real_part, imag_part = green_tiles(target_geo, source_geo, wavenum, weight)
        picked = jnp.take(values, cluster_ids, axis=1)
        picked = jnp.transpose(picked, (1, 0, 2)).reshape(-1, values.shape[2])
        swapped = jnp.concatenate([-picked[:, half_width:], picked[:, :half_width]], axis=1)
        result = jnp.dot(real_part[0], picked, preferred_element_type=jnp.float32)
        return result + jnp.dot(imag_part[0], swapped, preferred_element_type=jnp.float32)
    stacked = lax.map(one_cluster, jnp.arange(clusters_all, dtype=jnp.int32))
    return jnp.transpose(stacked, (1, 0, 2))

def reference(charges, geometry, wavenumber, requests, pairs, counts):
    first = apply_operator(charges, geometry, wavenumber, requests, pairs, counts)
    iterate = (charges.astype(jnp.float32) - first).astype(jnp.bfloat16)
    image = apply_operator(iterate, geometry, wavenumber, requests, pairs, counts)
    return (iterate, image)
```

```python
import functools

import jax
import jax.numpy as jnp
from jax import lax
from jax.experimental import pallas as pl
from jax.experimental.pallas import tpu as pltpu
from jax.sharding import PartitionSpec as P

CPD = 12
CAP = 4
PPT = 32

quarter_turn = 0.7853981633974483
two_pi = 6.283185307179586
inverse_four_pi = 0.07957747154594767
two_over_pi = 0.6366197723675814

STRIP = 16
LANES = 128


def sincos(x):
    n = jnp.floor(x * two_over_pi + 0.5)
    r = ((x - n * 1.5703125) - n * 4.837512969970703125e-4) - n * 7.54978995489188216e-8
    z = r * r
    s = ((-1.9515295891e-4 * z + 8.3321608736e-3) * z - 1.6666654611e-1) * z * r + r
    c = ((2.443315711809948e-5 * z - 1.388731625493765e-3) * z + 4.166664568298827e-2) * z * z
    c = c - 0.5 * z + 1.0
    q = n.astype(jnp.int32)
    swap = (q & 1) == 1
    s0 = jnp.where(swap, c, s)
    c0 = jnp.where(swap, s, c)
    sin = jnp.where((q & 2) == 2, -s0, s0)
    cos = jnp.where(((q + 1) & 2) == 2, -c0, c0)
    return sin, cos


def green(k, xt, yt, zt, et, xs, ys, zs, area, sj, cj):
    dx = xt - xs
    dy = yt - ys
    planar = dx * dx + dy * dy
    dz = zt - zs
    zsum = zt + zs
    direct = lax.rsqrt(planar + dz * dz + area)
    mirror = lax.rsqrt(planar + zsum * zsum + area)
    kr = k * jnp.sqrt(planar)
    amp = (et * cj) * lax.rsqrt(1.0 + kr)
    sin, cos = sincos(kr + quarter_turn)
    return sj * (direct + mirror) - amp * sin, amp * cos


def tile_into(k, tb_ref, sb_ref, g, p, tr_ref, ti_ref):
    width = tr_ref.shape[0]
    halves = tr_ref.shape[1] // LANES
    for h in range(halves):
        lanes = pl.ds(h * LANES, LANES)
        xt = tb_ref[g, 0, :, lanes]
        yt = tb_ref[g, 1, :, lanes]
        zt = tb_ref[g, 2, :, lanes]
        et = tb_ref[g, 3, :, lanes]

        def strip(r, carry):
            rows = pl.ds(pl.multiple_of(r * STRIP, STRIP), STRIP)
            xs = sb_ref[p, 0, rows, :]
            ys = sb_ref[p, 1, rows, :]
            zs = sb_ref[p, 2, rows, :]
            area = sb_ref[p, 3, rows, :]
            sj = sb_ref[p, 4, rows, :]
            cj = sb_ref[p, 5, rows, :]
            re, im = green(k, xt, yt, zt, et, xs, ys, zs, area, sj, cj)
            tr_ref[rows, lanes] = re.astype(jnp.bfloat16)
            ti_ref[rows, lanes] = im.astype(jnp.bfloat16)
            return carry

        lax.fori_loop(0, width // STRIP, strip, 0)


def entry_product(l_ref, p, tr, ti):
    part = jnp.dot(l_ref[p, 0], tr, preferred_element_type=jnp.float32)
    return part + jnp.dot(l_ref[p, 1], ti, preferred_element_type=jnp.float32)


def first_kernel(n_ref, g_ref, p_ref, w_ref, k_ref, tb_ref, sb_ref, l_ref, acc_ref, tiles_hbm,
                 tbuf, sem):
    n = n_ref[0]
    k = k_ref[0]
    acc_ref[...] = jnp.zeros_like(acc_ref)

    def copy(e, slot):
        return pltpu.make_async_copy(tbuf.at[slot], tiles_hbm.at[e], sem.at[slot])

    def body(e, carry):
        slot = e % 2
        g = g_ref[e]
        p = p_ref[e]
        w = w_ref[e]

        @pl.when(e >= 2)
        def _():
            copy(e - 2, slot).wait()

        tile_into(k, tb_ref, sb_ref, g, p, tbuf.at[slot, 0], tbuf.at[slot, 1])
        copy(e, slot).start()
        part = entry_product(l_ref, p, tbuf[slot, 0], tbuf[slot, 1])
        acc_ref[g] = acc_ref[g] + w * part
        return carry

    lax.fori_loop(0, n, body, 0)

    @pl.when(n >= 2)
    def _():
        copy(n - 2, (n - 2) % 2).wait()

    @pl.when(n >= 1)
    def _():
        copy(n - 1, (n - 1) % 2).wait()


def second_kernel(n_ref, g_ref, p_ref, w_ref, l_ref, tiles_hbm, acc_ref, tbuf, sem):
    n = n_ref[0]
    acc_ref[...] = jnp.zeros_like(acc_ref)

    def copy(e, slot):
        return pltpu.make_async_copy(tiles_hbm.at[e], tbuf.at[slot], sem.at[slot])

    @pl.when(n >= 1)
    def _():
        copy(0, 0).start()

    def body(e, carry):
        slot = e % 2
        g = g_ref[e]
        p = p_ref[e]
        w = w_ref[e]
        copy(e, slot).wait()

        @pl.when(e + 1 < n)
        def _():
            copy(e + 1, 1 - slot).start()

        part = entry_product(l_ref, p, tbuf[slot, 0], tbuf[slot, 1])
        acc_ref[g] = acc_ref[g] + w * part
        return carry

    lax.fori_loop(0, n, body, 0)


SMEM_SPEC = pl.BlockSpec(memory_space=pltpu.SMEM)
VMEM_SPEC = pl.BlockSpec(memory_space=pltpu.VMEM)
ANY_SPEC = pl.BlockSpec(memory_space=pl.ANY)


def first_product(n, g_list, p_list, w_list, k, tb, sb, lhs):
    clusters = tb.shape[0]
    targets = tb.shape[3]
    nmax = g_list.shape[0]
    width = sb.shape[2]
    cols = lhs.shape[2]
    elems = nmax * width * targets
    return pl.pallas_call(
        first_kernel,
        out_shape=(
            jax.ShapeDtypeStruct((clusters, cols, targets), jnp.float32),
            jax.ShapeDtypeStruct((nmax, 2, width, targets), jnp.bfloat16),
        ),
        in_specs=[SMEM_SPEC] * 5 + [VMEM_SPEC] * 3,
        out_specs=(VMEM_SPEC, ANY_SPEC),
        scratch_shapes=[
            pltpu.VMEM((2, 2, width, targets), jnp.bfloat16),
            pltpu.SemaphoreType.DMA((2,)),
        ],
        cost_estimate=pl.CostEstimate(
            flops=elems * 60 + 4 * elems * cols,
            transcendentals=elems * 4,
            bytes_accessed=elems * 4,
        ),
    )(n, g_list, p_list, w_list, k, tb, sb, lhs)


def second_product(n, g_list, p_list, w_list, lhs, tiles, clusters):
    nmax, _, width, targets = tiles.shape
    cols = lhs.shape[2]
    elems = nmax * width * targets
    return pl.pallas_call(
        second_kernel,
        out_shape=jax.ShapeDtypeStruct((clusters, cols, targets), jnp.float32),
        in_specs=[SMEM_SPEC] * 4 + [VMEM_SPEC, ANY_SPEC],
        out_specs=VMEM_SPEC,
        scratch_shapes=[
            pltpu.VMEM((2, 2, width, targets), jnp.bfloat16),
            pltpu.SemaphoreType.DMA((2,)),
        ],
        cost_estimate=pl.CostEstimate(
            flops=4 * elems * cols, transcendentals=0, bytes_accessed=elems * 4
        ),
    )(n, g_list, p_list, w_list, lhs, tiles)


def local(charges, geometry, wavenumber, requests, pairs, counts):
    clus_index = lax.axis_index("clus")
    src_index = lax.axis_index("src")
    sub_index = lax.axis_index("sub")
    clus_count = lax.axis_size("clus")
    sub_count = lax.axis_size("sub")
    source_rows = charges.shape[0]
    share_rows = source_rows // sub_count
    targets = geometry.shape[2]
    cpd = charges.shape[1]
    wavenum = wavenumber[0]
    slot_total = clus_count * requests.shape[2]

    served = lax.all_to_all(requests[0], "clus", split_axis=0, concat_axis=0, tiled=True).reshape(
        -1
    )
    served_index = jnp.maximum(served, 0)
    served_mask = (served >= 0).astype(jnp.bfloat16)[None, :, None]

    def fetch(values):
        picked = jnp.take(values, served_index, axis=1) * served_mask
        return lax.all_to_all(picked, "clus", split_axis=1, concat_axis=1, tiled=True)

    def lhs_of(values):
        blocks = fetch(values)
        half_width = blocks.shape[2] // 2
        swapped = jnp.concatenate([-blocks[..., half_width:], blocks[..., :half_width]], axis=-1)
        return jnp.stack(
            [jnp.transpose(blocks, (1, 2, 0)), jnp.transpose(swapped, (1, 2, 0))], axis=1
        )

    target_geo = lax.dynamic_slice_in_dim(geometry, clus_index * cpd, cpd, axis=1)
    tq = jnp.stack(
        [target_geo[0], target_geo[1], target_geo[2], jnp.exp(wavenum * target_geo[2])], axis=1
    )
    tb = jnp.broadcast_to(tq[:, :, None, :], (cpd, 4, STRIP, targets))

    base_ids = jnp.arange(clus_count, dtype=jnp.int32)[:, None] * cpd
    source_ids = (base_ids + jnp.maximum(requests[0], 0)).reshape(-1)
    source_full = jnp.take(geometry, source_ids, axis=1)
    source_geo = lax.dynamic_slice_in_dim(source_full, src_index * source_rows, source_rows, axis=2)
    sj = source_geo[3] * inverse_four_pi
    cj = (two_pi * wavenum) * jnp.exp(wavenum * source_geo[2]) * sj
    sq = jnp.stack([source_geo[0], source_geo[1], source_geo[2], source_geo[3], sj, cj], axis=1)
    sb = jnp.broadcast_to(sq[..., None], sq.shape + (LANES,))

    slot_ids = pairs[:, 0, :]
    live = jnp.arange(pairs.shape[2], dtype=jnp.int32)[None, :] < counts[:, 0:1]
    hits = (slot_ids[:, :, None] == jnp.arange(slot_total, dtype=jnp.int32)[None, None, :]) & live[
        :, :, None
    ]
    weight = jnp.sum(hits.astype(jnp.int32), axis=1).reshape(-1)
    nmax = cpd * min(slot_total, pairs.shape[2])
    order = jnp.argsort((weight == 0).astype(jnp.int32), stable=True)[:nmax].astype(jnp.int32)
    g_list = order // slot_total
    p_list = order % slot_total
    w_list = jnp.take(weight, order).astype(jnp.float32)
    n = jnp.sum((weight > 0).astype(jnp.int32)).reshape(1)
    k_arr = wavenumber.astype(jnp.float32).reshape(1)

    def finish(acc):
        return lax.psum_scatter(
            jnp.transpose(acc, (2, 0, 1)), ("src", "sub"), scatter_dimension=0, tiled=True
        )

    acc, tiles = first_product(n, g_list, p_list, w_list, k_arr, tb, sb, lhs_of(charges))
    first = finish(acc)
    own_rows = lax.dynamic_slice_in_dim(charges, sub_index * share_rows, share_rows, axis=0)
    iterate_share = (own_rows.astype(jnp.float32) - first).astype(jnp.bfloat16)
    iterate = lax.all_gather(iterate_share, "sub", axis=0, tiled=True)
    acc2 = second_product(n, g_list, p_list, w_list, lhs_of(iterate), tiles, cpd)
    image = finish(acc2)
    return (iterate, image)


def solution(mesh):
    in_specs = (
        P(("freq", "src"), "clus", None),
        P(),
        P("freq"),
        P(("clus", "sub"), None, None),
        P("clus", "sub", None),
        P("clus", "sub"),
    )
    out_specs = (P(("freq", "src"), "clus", None), P(("freq", "src", "sub"), "clus", None))
    return jax.shard_map(local, mesh=mesh, in_specs=in_specs, out_specs=out_specs, check_vma=False)
```

```python
import jax
import jax.numpy as jnp
from jax import lax
from jax.experimental import pallas as pl
from jax.experimental.pallas import tpu as pltpu
from jax.sharding import PartitionSpec as P

CPD = 12
CAP = 4
PPT = 32

quarter_turn = 0.7853981633974483
two_pi = 6.283185307179586
inverse_four_pi = 0.07957747154594767
two_over_pi = 0.6366197723675814

STRIP = 16
LANES = 128


def sincos(x):
    n = jnp.floor(x * two_over_pi + 0.5)
    r = ((x - n * 1.5703125) - n * 4.837512969970703125e-4) - n * 7.54978995489188216e-8
    z = r * r
    s = ((-1.9515295891e-4 * z + 8.3321608736e-3) * z - 1.6666654611e-1) * z * r + r
    c = ((2.443315711809948e-5 * z - 1.388731625493765e-3) * z + 4.166664568298827e-2) * z * z
    c = c - 0.5 * z + 1.0
    q = n.astype(jnp.int32)
    swap = (q & 1) == 1
    s0 = jnp.where(swap, c, s)
    c0 = jnp.where(swap, s, c)
    sin = jnp.where((q & 2) == 2, -s0, s0)
    cos = jnp.where(((q + 1) & 2) == 2, -c0, c0)
    return sin, cos


def green(k, xt, yt, zt, et, xs, ys, zs, area, sj, cj):
    dx = xt - xs
    dy = yt - ys
    planar = dx * dx + dy * dy
    dz = zt - zs
    zsum = zt + zs
    direct = lax.rsqrt(planar + dz * dz + area)
    mirror = lax.rsqrt(planar + zsum * zsum + area)
    kr = k * jnp.sqrt(planar)
    amp = (et * cj) * lax.rsqrt(1.0 + kr)
    sin, cos = sincos(kr + quarter_turn)
    return sj * (direct + mirror) - amp * sin, amp * cos


def tile_into(k, tb_ref, sb_ref, g, p, tr_ref, ti_ref):
    width = tr_ref.shape[0]
    halves = tr_ref.shape[1] // LANES
    for h in range(halves):
        lanes = pl.ds(h * LANES, LANES)
        xt = tb_ref[g, 0, :, lanes]
        yt = tb_ref[g, 1, :, lanes]
        zt = tb_ref[g, 2, :, lanes]
        et = tb_ref[g, 3, :, lanes]

        def strip(r, carry):
            rows = pl.ds(pl.multiple_of(r * STRIP, STRIP), STRIP)
            xs = sb_ref[p, 0, rows, :]
            ys = sb_ref[p, 1, rows, :]
            zs = sb_ref[p, 2, rows, :]
            area = sb_ref[p, 3, rows, :]
            sj = sb_ref[p, 4, rows, :]
            cj = sb_ref[p, 5, rows, :]
            re, im = green(k, xt, yt, zt, et, xs, ys, zs, area, sj, cj)
            tr_ref[rows, lanes] = re.astype(jnp.bfloat16)
            ti_ref[rows, lanes] = im.astype(jnp.bfloat16)
            return carry

        lax.fori_loop(0, width // STRIP, strip, 0)


def entry_product(l_ref, p, tr, ti):
    part = jnp.dot(l_ref[p, 0], tr, preferred_element_type=jnp.float32)
    return part + jnp.dot(l_ref[p, 1], ti, preferred_element_type=jnp.float32)


def product_kernel(n_ref, g_ref, p_ref, w_ref, k_ref, tb_ref, sb_ref, l_ref, acc_ref, tbuf):
    n = n_ref[0]
    k = k_ref[0]
    acc_ref[...] = jnp.zeros_like(acc_ref)

    def body(e, carry):
        g = g_ref[e]
        p = p_ref[e]
        w = w_ref[e]
        tile_into(k, tb_ref, sb_ref, g, p, tbuf.at[0], tbuf.at[1])
        part = entry_product(l_ref, p, tbuf[0], tbuf[1])
        acc_ref[g] = acc_ref[g] + w * part
        return carry

    lax.fori_loop(0, n, body, 0)


SMEM_SPEC = pl.BlockSpec(memory_space=pltpu.SMEM)
VMEM_SPEC = pl.BlockSpec(memory_space=pltpu.VMEM)


def product(n, g_list, p_list, w_list, k, tb, sb, lhs):
    clusters = tb.shape[0]
    targets = tb.shape[3]
    nmax = g_list.shape[0]
    width = sb.shape[2]
    cols = lhs.shape[2]
    elems = nmax * width * targets
    return pl.pallas_call(
        product_kernel,
        out_shape=jax.ShapeDtypeStruct((clusters, cols, targets), jnp.float32),
        in_specs=[SMEM_SPEC] * 5 + [VMEM_SPEC] * 3,
        out_specs=VMEM_SPEC,
        scratch_shapes=[pltpu.VMEM((2, width, targets), jnp.bfloat16)],
        cost_estimate=pl.CostEstimate(
            flops=elems * 60 + 4 * elems * cols,
            transcendentals=elems * 4,
            bytes_accessed=elems * 2,
        ),
    )(n, g_list, p_list, w_list, k, tb, sb, lhs)


def local(charges, geometry, wavenumber, requests, pairs, counts):
    clus_index = lax.axis_index("clus")
    src_index = lax.axis_index("src")
    sub_index = lax.axis_index("sub")
    clus_count = lax.axis_size("clus")
    sub_count = lax.axis_size("sub")
    source_rows = charges.shape[0]
    share_rows = source_rows // sub_count
    targets = geometry.shape[2]
    cpd = charges.shape[1]
    wavenum = wavenumber[0]
    slot_total = clus_count * requests.shape[2]

    served = lax.all_to_all(requests[0], "clus", split_axis=0, concat_axis=0, tiled=True).reshape(
        -1
    )
    served_index = jnp.maximum(served, 0)
    served_mask = (served >= 0).astype(jnp.bfloat16)[None, :, None]

    def fetch(values):
        picked = jnp.take(values, served_index, axis=1) * served_mask
        return lax.all_to_all(picked, "clus", split_axis=1, concat_axis=1, tiled=True)

    def lhs_of(values):
        blocks = fetch(values)
        half_width = blocks.shape[2] // 2
        swapped = jnp.concatenate([-blocks[..., half_width:], blocks[..., :half_width]], axis=-1)
        return jnp.stack(
            [jnp.transpose(blocks, (1, 2, 0)), jnp.transpose(swapped, (1, 2, 0))], axis=1
        )

    target_geo = lax.dynamic_slice_in_dim(geometry, clus_index * cpd, cpd, axis=1)
    tq = jnp.stack(
        [target_geo[0], target_geo[1], target_geo[2], jnp.exp(wavenum * target_geo[2])], axis=1
    )
    tb = jnp.broadcast_to(tq[:, :, None, :], (cpd, 4, STRIP, targets))

    base_ids = jnp.arange(clus_count, dtype=jnp.int32)[:, None] * cpd
    source_ids = (base_ids + jnp.maximum(requests[0], 0)).reshape(-1)
    source_full = jnp.take(geometry, source_ids, axis=1)
    source_geo = lax.dynamic_slice_in_dim(source_full, src_index * source_rows, source_rows, axis=2)
    sj = source_geo[3] * inverse_four_pi
    cj = (two_pi * wavenum) * jnp.exp(wavenum * source_geo[2]) * sj
    sq = jnp.stack([source_geo[0], source_geo[1], source_geo[2], source_geo[3], sj, cj], axis=1)
    sb = jnp.broadcast_to(sq[..., None], sq.shape + (LANES,))

    slot_ids = pairs[:, 0, :]
    live = jnp.arange(pairs.shape[2], dtype=jnp.int32)[None, :] < counts[:, 0:1]
    hits = (slot_ids[:, :, None] == jnp.arange(slot_total, dtype=jnp.int32)[None, None, :]) & live[
        :, :, None
    ]
    weight = jnp.sum(hits.astype(jnp.int32), axis=1).reshape(-1)
    nmax = cpd * min(slot_total, pairs.shape[2])
    order = jnp.argsort((weight == 0).astype(jnp.int32), stable=True)[:nmax].astype(jnp.int32)
    g_list = order // slot_total
    p_list = order % slot_total
    w_list = jnp.take(weight, order).astype(jnp.float32)
    n = jnp.sum((weight > 0).astype(jnp.int32)).reshape(1)
    k_arr = wavenumber.astype(jnp.float32).reshape(1)

    def finish(acc):
        return lax.psum_scatter(
            jnp.transpose(acc, (2, 0, 1)), ("src", "sub"), scatter_dimension=0, tiled=True
        )

    first = finish(product(n, g_list, p_list, w_list, k_arr, tb, sb, lhs_of(charges)))
    own_rows = lax.dynamic_slice_in_dim(charges, sub_index * share_rows, share_rows, axis=0)
    iterate_share = (own_rows.astype(jnp.float32) - first).astype(jnp.bfloat16)
    iterate = lax.all_gather(iterate_share, "sub", axis=0, tiled=True)
    image = finish(product(n, g_list, p_list, w_list, k_arr, tb, sb, lhs_of(iterate)))
    return (iterate, image)


def solution(mesh):
    in_specs = (
        P(("freq", "src"), "clus", None),
        P(),
        P("freq"),
        P(("clus", "sub"), None, None),
        P("clus", "sub", None),
        P("clus", "sub"),
    )
    out_specs = (P(("freq", "src"), "clus", None), P(("freq", "src", "sub"), "clus", None))
    return jax.shard_map(local, mesh=mesh, in_specs=in_specs, out_specs=out_specs, check_vma=False)
```

```python
import jax
import jax.numpy as jnp
from jax import lax
from jax.experimental import pallas as pl
from jax.experimental.pallas import tpu as pltpu
from jax.sharding import PartitionSpec as P

CPD = 12
CAP = 4
PPT = 32

quarter_turn = 0.7853981633974483
two_pi = 6.283185307179586
inverse_four_pi = 0.07957747154594767
two_over_pi = 0.6366197723675814

STRIP = 16
LANES = 128
UNROLL = 2


def sincos(x):
    n = jnp.floor(x * two_over_pi + 0.5)
    r = (x - n * 1.5703125) - n * 4.838267923332751e-4
    z = r * r
    s = ((-1.9515295891e-4 * z + 8.3321608736e-3) * z - 1.6666654611e-1) * z * r + r
    c = ((2.443315711809948e-5 * z - 1.388731625493765e-3) * z + 4.166664568298827e-2) * z * z
    c = c - 0.5 * z + 1.0
    q = n.astype(jnp.int32)
    swap = (q & 1) == 1
    s0 = jnp.where(swap, c, s)
    c0 = jnp.where(swap, s, c)
    sin = jnp.where((q & 2) == 2, -s0, s0)
    cos = jnp.where(((q + 1) & 2) == 2, -c0, c0)
    return sin, cos


def green(k, xt, yt, zt, zt4, et, xs, ys, zs, area, sj, cj):
    dx = xt - xs
    dy = yt - ys
    planar = dx * dx + dy * dy
    dz = zt - zs
    near = planar + dz * dz + area
    direct = lax.rsqrt(near)
    mirror = lax.rsqrt(near + zt4 * zs)
    kr = k * jnp.sqrt(planar)
    amp = (et * cj) * lax.rsqrt(1.0 + kr)
    sin, cos = sincos(kr + quarter_turn)
    return sj * (direct + mirror) - amp * sin, amp * cos


def tile_into(k, tb_ref, sb_ref, g, p, tr_ref, ti_ref):
    width = tr_ref.shape[0]
    halves = tr_ref.shape[1] // LANES

    def strip(r, carry):
        rows = pl.ds(pl.multiple_of(r * STRIP, STRIP), STRIP)
        xs = sb_ref[p, 0, rows, :]
        ys = sb_ref[p, 1, rows, :]
        zs = sb_ref[p, 2, rows, :]
        area = sb_ref[p, 3, rows, :]
        sj = sb_ref[p, 4, rows, :]
        cj = sb_ref[p, 5, rows, :]
        for h in range(halves):
            lanes = pl.ds(h * LANES, LANES)
            xt = tb_ref[g, 0, :, lanes]
            yt = tb_ref[g, 1, :, lanes]
            zt = tb_ref[g, 2, :, lanes]
            et = tb_ref[g, 3, :, lanes]
            zt4 = tb_ref[g, 4, :, lanes]
            re, im = green(k, xt, yt, zt, zt4, et, xs, ys, zs, area, sj, cj)
            tr_ref[rows, lanes] = re.astype(jnp.bfloat16)
            ti_ref[rows, lanes] = im.astype(jnp.bfloat16)
        return carry

    lax.fori_loop(0, width // STRIP, strip, 0, unroll=UNROLL)


def entry_product(l_ref, p, tr, ti):
    part = jnp.dot(l_ref[p, 0], tr, preferred_element_type=jnp.float32)
    return part + jnp.dot(l_ref[p, 1], ti, preferred_element_type=jnp.float32)


def product_kernel(n_ref, g_ref, p_ref, w_ref, k_ref, tb_ref, sb_ref, l_ref, acc_ref, tbuf):
    n = n_ref[0]
    k = k_ref[0]
    acc_ref[...] = jnp.zeros_like(acc_ref)

    def body(e, carry):
        g = g_ref[e]
        p = p_ref[e]
        w = w_ref[e]
        tile_into(k, tb_ref, sb_ref, g, p, tbuf.at[0], tbuf.at[1])
        part = entry_product(l_ref, p, tbuf[0], tbuf[1])
        acc_ref[g] = acc_ref[g] + w * part
        return carry

    lax.fori_loop(0, n, body, 0)


SMEM_SPEC = pl.BlockSpec(memory_space=pltpu.SMEM)
VMEM_SPEC = pl.BlockSpec(memory_space=pltpu.VMEM)


def product(n, g_list, p_list, w_list, k, tb, sb, lhs):
    clusters = tb.shape[0]
    targets = tb.shape[3]
    nmax = g_list.shape[0]
    width = sb.shape[2]
    cols = lhs.shape[2]
    elems = nmax * width * targets
    return pl.pallas_call(
        product_kernel,
        out_shape=jax.ShapeDtypeStruct((clusters, cols, targets), jnp.float32),
        in_specs=[SMEM_SPEC] * 5 + [VMEM_SPEC] * 3,
        out_specs=VMEM_SPEC,
        scratch_shapes=[pltpu.VMEM((2, width, targets), jnp.bfloat16)],
        cost_estimate=pl.CostEstimate(
            flops=elems * 60 + 4 * elems * cols,
            transcendentals=elems * 4,
            bytes_accessed=elems * 2,
        ),
    )(n, g_list, p_list, w_list, k, tb, sb, lhs)


def local(charges, geometry, wavenumber, requests, pairs, counts):
    clus_index = lax.axis_index("clus")
    src_index = lax.axis_index("src")
    sub_index = lax.axis_index("sub")
    clus_count = lax.axis_size("clus")
    sub_count = lax.axis_size("sub")
    source_rows = charges.shape[0]
    share_rows = source_rows // sub_count
    targets = geometry.shape[2]
    cpd = charges.shape[1]
    wavenum = wavenumber[0]
    slot_total = clus_count * requests.shape[2]

    served = lax.all_to_all(requests[0], "clus", split_axis=0, concat_axis=0, tiled=True).reshape(
        -1
    )
    served_index = jnp.maximum(served, 0)
    served_mask = (served >= 0).astype(jnp.bfloat16)[None, :, None]

    def fetch(values):
        picked = jnp.take(values, served_index, axis=1) * served_mask
        return lax.all_to_all(picked, "clus", split_axis=1, concat_axis=1, tiled=True)

    def lhs_of(values):
        blocks = fetch(values)
        half_width = blocks.shape[2] // 2
        swapped = jnp.concatenate([-blocks[..., half_width:], blocks[..., :half_width]], axis=-1)
        return jnp.stack(
            [jnp.transpose(blocks, (1, 2, 0)), jnp.transpose(swapped, (1, 2, 0))], axis=1
        )

    target_geo = lax.dynamic_slice_in_dim(geometry, clus_index * cpd, cpd, axis=1)
    tq = jnp.stack(
        [
            target_geo[0],
            target_geo[1],
            target_geo[2],
            jnp.exp(wavenum * target_geo[2]),
            4.0 * target_geo[2],
        ],
        axis=1,
    )
    tb = jnp.broadcast_to(tq[:, :, None, :], (cpd, tq.shape[1], STRIP, targets))

    base_ids = jnp.arange(clus_count, dtype=jnp.int32)[:, None] * cpd
    source_ids = (base_ids + jnp.maximum(requests[0], 0)).reshape(-1)
    source_full = jnp.take(geometry, source_ids, axis=1)
    source_geo = lax.dynamic_slice_in_dim(source_full, src_index * source_rows, source_rows, axis=2)
    sj = source_geo[3] * inverse_four_pi
    cj = (two_pi * wavenum) * jnp.exp(wavenum * source_geo[2]) * sj
    sq = jnp.stack([source_geo[0], source_geo[1], source_geo[2], source_geo[3], sj, cj], axis=1)
    sb = jnp.broadcast_to(sq[..., None], sq.shape + (LANES,))

    slot_ids = pairs[:, 0, :]
    live = jnp.arange(pairs.shape[2], dtype=jnp.int32)[None, :] < counts[:, 0:1]
    hits = (slot_ids[:, :, None] == jnp.arange(slot_total, dtype=jnp.int32)[None, None, :]) & live[
        :, :, None
    ]
    weight = jnp.sum(hits.astype(jnp.int32), axis=1).reshape(-1)
    nmax = cpd * min(slot_total, pairs.shape[2])
    order = jnp.argsort((weight == 0).astype(jnp.int32), stable=True)[:nmax].astype(jnp.int32)
    g_list = order // slot_total
    p_list = order % slot_total
    w_list = jnp.take(weight, order).astype(jnp.float32)
    n = jnp.sum((weight > 0).astype(jnp.int32)).reshape(1)
    k_arr = wavenumber.astype(jnp.float32).reshape(1)

    def finish(acc):
        return lax.psum_scatter(
            jnp.transpose(acc, (2, 0, 1)), ("src", "sub"), scatter_dimension=0, tiled=True
        )

    first = finish(product(n, g_list, p_list, w_list, k_arr, tb, sb, lhs_of(charges)))
    own_rows = lax.dynamic_slice_in_dim(charges, sub_index * share_rows, share_rows, axis=0)
    iterate_share = (own_rows.astype(jnp.float32) - first).astype(jnp.bfloat16)
    iterate = lax.all_gather(iterate_share, "sub", axis=0, tiled=True)
    image = finish(product(n, g_list, p_list, w_list, k_arr, tb, sb, lhs_of(iterate)))
    return (iterate, image)


def solution(mesh):
    in_specs = (
        P(("freq", "src"), "clus", None),
        P(),
        P("freq"),
        P(("clus", "sub"), None, None),
        P("clus", "sub", None),
        P("clus", "sub"),
    )
    out_specs = (P(("freq", "src"), "clus", None), P(("freq", "src", "sub"), "clus", None))
    return jax.shard_map(local, mesh=mesh, in_specs=in_specs, out_specs=out_specs, check_vma=False)
```

```python
import jax
import jax.numpy as jnp
from jax import lax
from jax.experimental import pallas as pl
from jax.experimental.pallas import tpu as pltpu
from jax.sharding import PartitionSpec as P

CPD = 12
CAP = 4
PPT = 32

quarter_turn = 0.7853981633974483
two_pi = 6.283185307179586
inverse_four_pi = 0.07957747154594767
two_over_pi = 0.6366197723675814

STRIP = 16
LANES = 128
UNROLL = 2


def sincos(x):
    n = jnp.floor(x * two_over_pi + 0.5)
    r = (x - n * 1.5703125) - n * 4.838267923332751e-4
    z = r * r
    s = ((-1.9515295891e-4 * z + 8.3321608736e-3) * z - 1.6666654611e-1) * z * r + r
    c = ((2.443315711809948e-5 * z - 1.388731625493765e-3) * z + 4.166664568298827e-2) * z * z
    c = c - 0.5 * z + 1.0
    q = n.astype(jnp.int32)
    swap = (q & 1) == 1
    s0 = jnp.where(swap, c, s)
    c0 = jnp.where(swap, s, c)
    sin = jnp.where((q & 2) == 2, -s0, s0)
    cos = jnp.where(((q + 1) & 2) == 2, -c0, c0)
    return sin, cos


def green(k, xt, yt, zt, zt4, et, xs, ys, zs, area, sj, cj):
    dx = xt - xs
    dy = yt - ys
    planar = dx * dx + dy * dy
    dz = zt - zs
    near = planar + dz * dz + area
    direct = lax.rsqrt(near)
    mirror = lax.rsqrt(near + zt4 * zs)
    kr = k * jnp.sqrt(planar)
    amp = (et * cj) * lax.rsqrt(1.0 + kr)
    sin, cos = sincos(kr + quarter_turn)
    return sj * (direct + mirror) - amp * sin, amp * cos


def tile_into(k, tb_ref, sb_ref, g, p, tr_ref, ti_ref):
    width = tr_ref.shape[0]
    halves = tr_ref.shape[1] // LANES

    def strip(r, carry):
        rows = pl.ds(pl.multiple_of(r * STRIP, STRIP), STRIP)
        xs = sb_ref[p, 0, rows, :]
        ys = sb_ref[p, 1, rows, :]
        zs = sb_ref[p, 2, rows, :]
        area = sb_ref[p, 3, rows, :]
        sj = sb_ref[p, 4, rows, :]
        cj = sb_ref[p, 5, rows, :]
        for h in range(halves):
            lanes = pl.ds(h * LANES, LANES)
            xt = tb_ref[g, 0, :, lanes]
            yt = tb_ref[g, 1, :, lanes]
            zt = tb_ref[g, 2, :, lanes]
            et = tb_ref[g, 3, :, lanes]
            zt4 = tb_ref[g, 4, :, lanes]
            re, im = green(k, xt, yt, zt, zt4, et, xs, ys, zs, area, sj, cj)
            tr_ref[rows, lanes] = re.astype(jnp.bfloat16)
            ti_ref[rows, lanes] = im.astype(jnp.bfloat16)
        return carry

    lax.fori_loop(0, width // STRIP, strip, 0, unroll=UNROLL)


def entry_product(l_ref, p, tile):
    return jnp.dot(l_ref[p], tile, preferred_element_type=jnp.float32)


def product_kernel(n_ref, g_ref, p_ref, w_ref, k_ref, tb_ref, sb_ref, l_ref, acc_ref, tbuf):
    n = n_ref[0]
    k = k_ref[0]
    acc_ref[...] = jnp.zeros_like(acc_ref)

    def body(e, carry):
        g = g_ref[e]
        p = p_ref[e]
        w = w_ref[e]
        width = tbuf.shape[0] // 2
        tile_into(k, tb_ref, sb_ref, g, p, tbuf.at[pl.ds(0, width)], tbuf.at[pl.ds(width, width)])
        part = entry_product(l_ref, p, tbuf[...])
        acc_ref[g] = acc_ref[g] + w * part
        return carry

    lax.fori_loop(0, n, body, 0)


SMEM_SPEC = pl.BlockSpec(memory_space=pltpu.SMEM)
VMEM_SPEC = pl.BlockSpec(memory_space=pltpu.VMEM)


def product(n, g_list, p_list, w_list, k, tb, sb, lhs):
    clusters = tb.shape[0]
    targets = tb.shape[3]
    nmax = g_list.shape[0]
    width = sb.shape[2]
    cols = lhs.shape[1]
    elems = nmax * width * targets
    return pl.pallas_call(
        product_kernel,
        out_shape=jax.ShapeDtypeStruct((clusters, cols, targets), jnp.float32),
        in_specs=[SMEM_SPEC] * 5 + [VMEM_SPEC] * 3,
        out_specs=VMEM_SPEC,
        scratch_shapes=[pltpu.VMEM((2 * width, targets), jnp.bfloat16)],
        cost_estimate=pl.CostEstimate(
            flops=elems * 60 + 4 * elems * cols,
            transcendentals=elems * 4,
            bytes_accessed=elems * 2,
        ),
    )(n, g_list, p_list, w_list, k, tb, sb, lhs)


def scatter_sum(x, axis):
    count = lax.axis_size(axis)
    if count == 1:
        return x
    me = lax.axis_index(axis)
    blocks = x.reshape((count, x.shape[0] // count) + x.shape[1:])
    total = lax.dynamic_index_in_dim(blocks, me, 0, keepdims=False)
    for shift in range(1, count):
        send = lax.dynamic_index_in_dim(blocks, (me + shift) % count, 0, keepdims=False)
        perm = [(i, (i + shift) % count) for i in range(count)]
        total = total + lax.ppermute(send, axis, perm=perm)
    return total


def local(charges, geometry, wavenumber, requests, pairs, counts):
    clus_index = lax.axis_index("clus")
    src_index = lax.axis_index("src")
    sub_index = lax.axis_index("sub")
    clus_count = lax.axis_size("clus")
    sub_count = lax.axis_size("sub")
    source_rows = charges.shape[0]
    share_rows = source_rows // sub_count
    targets = geometry.shape[2]
    cpd = charges.shape[1]
    wavenum = wavenumber[0]
    slot_total = clus_count * requests.shape[2]

    served = lax.all_to_all(requests[0], "clus", split_axis=0, concat_axis=0, tiled=True).reshape(
        -1
    )
    served_index = jnp.maximum(served, 0)
    served_mask = (served >= 0).astype(jnp.bfloat16)[None, :, None]

    def fetch(values):
        picked = jnp.take(values, served_index, axis=1) * served_mask
        return lax.all_to_all(picked, "clus", split_axis=1, concat_axis=1, tiled=True)

    def lhs_of(values):
        blocks = fetch(values)
        half_width = blocks.shape[2] // 2
        swapped = jnp.concatenate([-blocks[..., half_width:], blocks[..., :half_width]], axis=-1)
        return jnp.concatenate(
            [jnp.transpose(blocks, (1, 2, 0)), jnp.transpose(swapped, (1, 2, 0))], axis=2
        )

    target_geo = lax.dynamic_slice_in_dim(geometry, clus_index * cpd, cpd, axis=1)
    tq = jnp.stack(
        [
            target_geo[0],
            target_geo[1],
            target_geo[2],
            jnp.exp(wavenum * target_geo[2]),
            4.0 * target_geo[2],
        ],
        axis=1,
    )
    tb = jnp.broadcast_to(tq[:, :, None, :], (cpd, tq.shape[1], STRIP, targets))

    base_ids = jnp.arange(clus_count, dtype=jnp.int32)[:, None] * cpd
    source_ids = (base_ids + jnp.maximum(requests[0], 0)).reshape(-1)
    source_full = jnp.take(geometry, source_ids, axis=1)
    source_geo = lax.dynamic_slice_in_dim(source_full, src_index * source_rows, source_rows, axis=2)
    sj = source_geo[3] * inverse_four_pi
    cj = (two_pi * wavenum) * jnp.exp(wavenum * source_geo[2]) * sj
    sq = jnp.stack([source_geo[0], source_geo[1], source_geo[2], source_geo[3], sj, cj], axis=1)
    sb = jnp.broadcast_to(sq[..., None], sq.shape + (LANES,))

    slot_ids = pairs[:, 0, :]
    live = jnp.arange(pairs.shape[2], dtype=jnp.int32)[None, :] < counts[:, 0:1]
    hits = (slot_ids[:, :, None] == jnp.arange(slot_total, dtype=jnp.int32)[None, None, :]) & live[
        :, :, None
    ]
    weight = jnp.sum(hits.astype(jnp.int32), axis=1).reshape(-1)
    nmax = cpd * min(slot_total, pairs.shape[2])
    order = jnp.argsort((weight == 0).astype(jnp.int32), stable=True)[:nmax].astype(jnp.int32)
    g_list = order // slot_total
    p_list = order % slot_total
    w_list = jnp.take(weight, order).astype(jnp.float32)
    n = jnp.sum((weight > 0).astype(jnp.int32)).reshape(1)
    k_arr = wavenumber.astype(jnp.float32).reshape(1)

    def finish(acc):
        return scatter_sum(scatter_sum(jnp.transpose(acc, (2, 0, 1)), "src"), "sub")

    first = finish(product(n, g_list, p_list, w_list, k_arr, tb, sb, lhs_of(charges)))
    own_rows = lax.dynamic_slice_in_dim(charges, sub_index * share_rows, share_rows, axis=0)
    iterate_share = (own_rows.astype(jnp.float32) - first).astype(jnp.bfloat16)
    iterate = lax.all_gather(iterate_share, "sub", axis=0, tiled=True)
    image = finish(product(n, g_list, p_list, w_list, k_arr, tb, sb, lhs_of(iterate)))
    return (iterate, image)


def solution(mesh):
    in_specs = (
        P(("freq", "src"), "clus", None),
        P(),
        P("freq"),
        P(("clus", "sub"), None, None),
        P("clus", "sub", None),
        P("clus", "sub"),
    )
    out_specs = (P(("freq", "src"), "clus", None), P(("freq", "src", "sub"), "clus", None))
    return jax.shard_map(local, mesh=mesh, in_specs=in_specs, out_specs=out_specs, check_vma=False)
```

```python
import jax
import jax.numpy as jnp
from jax import lax
from jax.experimental import pallas as pl
from jax.experimental.pallas import tpu as pltpu
from jax.sharding import PartitionSpec as P

CPD = 12
CAP = 4
PPT = 32

quarter_turn = 0.7853981633974483
two_pi = 6.283185307179586
inverse_four_pi = 0.07957747154594767
two_over_pi = 0.6366197723675814

STRIP = 16
LANES = 128
UNROLL = 2


def sincos(x):
    n = jnp.floor(x * two_over_pi + 0.5)
    r = (x - n * 1.5703125) - n * 4.838267923332751e-4
    z = r * r
    s = ((-1.9515295891e-4 * z + 8.3321608736e-3) * z - 1.6666654611e-1) * z * r + r
    c = ((2.443315711809948e-5 * z - 1.388731625493765e-3) * z + 4.166664568298827e-2) * z * z
    c = c - 0.5 * z + 1.0
    q = n.astype(jnp.int32)
    swap = (q & 1) == 1
    s0 = jnp.where(swap, c, s)
    c0 = jnp.where(swap, s, c)
    sin = jnp.where((q & 2) == 2, -s0, s0)
    cos = jnp.where(((q + 1) & 2) == 2, -c0, c0)
    return sin, cos


def green(k, xt, yt, zt, zt4, et, xs, ys, zs, area, sj, cj):
    dx = xt - xs
    dy = yt - ys
    planar = dx * dx + dy * dy
    dz = zt - zs
    near = planar + dz * dz + area
    direct = lax.rsqrt(near)
    mirror = lax.rsqrt(near + zt4 * zs)
    kr = k * jnp.sqrt(planar)
    amp = (et * cj) * lax.rsqrt(1.0 + kr)
    sin, cos = sincos(kr + quarter_turn)
    return sj * (direct + mirror) - amp * sin, amp * cos


def tile_into(k, tb_ref, sb_ref, g, p, tr_ref, ti_ref):
    width = tr_ref.shape[0]
    halves = tr_ref.shape[1] // LANES

    def strip(r, carry):
        rows = pl.ds(pl.multiple_of(r * STRIP, STRIP), STRIP)
        xs = sb_ref[p, 0, rows, :]
        ys = sb_ref[p, 1, rows, :]
        zs = sb_ref[p, 2, rows, :]
        area = sb_ref[p, 3, rows, :]
        sj = sb_ref[p, 4, rows, :]
        cj = sb_ref[p, 5, rows, :]
        for h in range(halves):
            lanes = pl.ds(h * LANES, LANES)
            xt = tb_ref[g, 0, :, lanes]
            yt = tb_ref[g, 1, :, lanes]
            zt = tb_ref[g, 2, :, lanes]
            et = tb_ref[g, 3, :, lanes]
            zt4 = tb_ref[g, 4, :, lanes]
            re, im = green(k, xt, yt, zt, zt4, et, xs, ys, zs, area, sj, cj)
            tr_ref[rows, lanes] = re.astype(jnp.bfloat16)
            ti_ref[rows, lanes] = im.astype(jnp.bfloat16)
        return carry

    lax.fori_loop(0, width // STRIP, strip, 0, unroll=UNROLL)


def entry_product(l_ref, p, tile):
    return jnp.dot(l_ref[p], tile, preferred_element_type=jnp.float32)


def product_kernel(n_ref, g_ref, p_ref, w_ref, k_ref, tb_ref, sb_ref, l_ref, acc_ref, tbuf):
    start = n_ref[0]
    stop = n_ref[1]
    k = k_ref[0]
    acc_ref[...] = jnp.zeros_like(acc_ref)

    def body(e, carry):
        g = g_ref[e]
        p = p_ref[e]
        w = w_ref[e]
        width = tbuf.shape[0] // 2
        tile_into(k, tb_ref, sb_ref, g, p, tbuf.at[pl.ds(0, width)], tbuf.at[pl.ds(width, width)])
        part = entry_product(l_ref, p, tbuf[...])
        acc_ref[g] = acc_ref[g] + w * part
        return carry

    lax.fori_loop(start, stop, body, 0)


SMEM_SPEC = pl.BlockSpec(memory_space=pltpu.SMEM)
VMEM_SPEC = pl.BlockSpec(memory_space=pltpu.VMEM)


def product(n, g_list, p_list, w_list, k, tb, sb, lhs):
    clusters = tb.shape[0]
    targets = tb.shape[3]
    nmax = g_list.shape[0]
    width = sb.shape[2]
    cols = lhs.shape[1]
    elems = nmax * width * targets
    return pl.pallas_call(
        product_kernel,
        out_shape=jax.ShapeDtypeStruct((clusters, cols, targets), jnp.float32),
        in_specs=[SMEM_SPEC] * 5 + [VMEM_SPEC] * 3,
        out_specs=VMEM_SPEC,
        scratch_shapes=[pltpu.VMEM((2 * width, targets), jnp.bfloat16)],
        cost_estimate=pl.CostEstimate(
            flops=elems * 60 + 4 * elems * cols,
            transcendentals=elems * 4,
            bytes_accessed=elems * 2,
        ),
    )(n, g_list, p_list, w_list, k, tb, sb, lhs)


def scatter_sum(x, axis):
    count = lax.axis_size(axis)
    if count == 1:
        return x
    me = lax.axis_index(axis)
    blocks = x.reshape((count, x.shape[0] // count) + x.shape[1:])
    total = lax.dynamic_index_in_dim(blocks, me, 0, keepdims=False)
    for shift in range(1, count):
        send = lax.dynamic_index_in_dim(blocks, (me + shift) % count, 0, keepdims=False)
        perm = [(i, (i + shift) % count) for i in range(count)]
        total = total + lax.ppermute(send, axis, perm=perm)
    return total


def local(charges, geometry, wavenumber, requests, pairs, counts):
    clus_index = lax.axis_index("clus")
    src_index = lax.axis_index("src")
    sub_index = lax.axis_index("sub")
    clus_count = lax.axis_size("clus")
    sub_count = lax.axis_size("sub")
    source_rows = charges.shape[0]
    share_rows = source_rows // sub_count
    targets = geometry.shape[2]
    cpd = charges.shape[1]
    wavenum = wavenumber[0]
    slot_total = clus_count * requests.shape[2]

    served = lax.all_to_all(requests[0], "clus", split_axis=0, concat_axis=0, tiled=True).reshape(
        -1
    )
    served_index = jnp.maximum(served, 0)
    served_mask = (served >= 0).astype(jnp.bfloat16)[None, :, None]

    def fetch(values):
        picked = jnp.take(values, served_index, axis=1) * served_mask
        return lax.all_to_all(picked, "clus", split_axis=1, concat_axis=1, tiled=True)

    def lhs_of(values):
        blocks = lax.all_gather(fetch(values), "sub", axis=1, tiled=True)
        half_width = blocks.shape[2] // 2
        swapped = jnp.concatenate([-blocks[..., half_width:], blocks[..., :half_width]], axis=-1)
        return jnp.concatenate(
            [jnp.transpose(blocks, (1, 2, 0)), jnp.transpose(swapped, (1, 2, 0))], axis=2
        )

    target_geo = lax.dynamic_slice_in_dim(geometry, clus_index * cpd, cpd, axis=1)
    tq = jnp.stack(
        [
            target_geo[0],
            target_geo[1],
            target_geo[2],
            jnp.exp(wavenum * target_geo[2]),
            4.0 * target_geo[2],
        ],
        axis=1,
    )
    tb = jnp.broadcast_to(tq[:, :, None, :], (cpd, tq.shape[1], STRIP, targets))

    slot_ids = pairs[:, 0, :]
    live = jnp.arange(pairs.shape[2], dtype=jnp.int32)[None, :] < counts[:, 0:1]
    hits = (slot_ids[:, :, None] == jnp.arange(slot_total, dtype=jnp.int32)[None, None, :]) & live[
        :, :, None
    ]
    weight = jnp.sum(hits.astype(jnp.int32), axis=1).reshape(-1)

    own_table = jnp.concatenate([requests[0].reshape(-1), weight])
    tables = lax.all_gather(own_table, "sub", axis=0, tiled=False)
    request_count = requests[0].size
    requests_all = tables[:, :request_count].reshape((sub_count,) + requests[0].shape)
    weight_all = tables[:, request_count:].reshape(-1)

    base_ids = jnp.arange(clus_count, dtype=jnp.int32)[None, :, None] * cpd
    source_ids = (base_ids + jnp.maximum(requests_all, 0)).reshape(-1)
    source_full = jnp.take(geometry, source_ids, axis=1)
    source_geo = lax.dynamic_slice_in_dim(source_full, src_index * source_rows, source_rows, axis=2)
    sj = source_geo[3] * inverse_four_pi
    cj = (two_pi * wavenum) * jnp.exp(wavenum * source_geo[2]) * sj
    sq = jnp.stack([source_geo[0], source_geo[1], source_geo[2], source_geo[3], sj, cj], axis=1)
    sb = jnp.broadcast_to(sq[..., None], sq.shape + (LANES,))

    per_half = cpd * slot_total
    nmax = sub_count * cpd * min(slot_total, pairs.shape[2])
    order = jnp.argsort((weight_all == 0).astype(jnp.int32), stable=True)[:nmax].astype(jnp.int32)
    half_of = order // per_half
    g_list = (order % per_half) // slot_total
    p_list = half_of * slot_total + order % slot_total
    w_list = jnp.take(weight_all, order).astype(jnp.float32)
    total = jnp.sum((weight_all > 0).astype(jnp.int32))
    share = (total + sub_count - 1) // sub_count
    begin = jnp.minimum(sub_index * share, total)
    n = jnp.stack([begin, jnp.minimum(begin + share, total)])
    k_arr = wavenumber.astype(jnp.float32).reshape(1)

    def finish(acc):
        return scatter_sum(scatter_sum(jnp.transpose(acc, (2, 0, 1)), "src"), "sub")

    first = finish(product(n, g_list, p_list, w_list, k_arr, tb, sb, lhs_of(charges)))
    own_rows = lax.dynamic_slice_in_dim(charges, sub_index * share_rows, share_rows, axis=0)
    iterate_share = (own_rows.astype(jnp.float32) - first).astype(jnp.bfloat16)
    iterate = lax.all_gather(iterate_share, "sub", axis=0, tiled=True)
    image = finish(product(n, g_list, p_list, w_list, k_arr, tb, sb, lhs_of(iterate)))
    return (iterate, image)


def solution(mesh):
    in_specs = (
        P(("freq", "src"), "clus", None),
        P(),
        P("freq"),
        P(("clus", "sub"), None, None),
        P("clus", "sub", None),
        P("clus", "sub"),
    )
    out_specs = (P(("freq", "src"), "clus", None), P(("freq", "src", "sub"), "clus", None))
    return jax.shard_map(local, mesh=mesh, in_specs=in_specs, out_specs=out_specs, check_vma=False)
```

```python
import jax
import jax.numpy as jnp
from jax import lax
from jax.experimental import pallas as pl
from jax.experimental.pallas import tpu as pltpu
from jax.sharding import PartitionSpec as P

CPD = 12
CAP = 4
PPT = 32

quarter_turn = 0.7853981633974483
two_pi = 6.283185307179586
inverse_four_pi = 0.07957747154594767
two_over_pi = 0.6366197723675814

STRIP = 16
LANES = 128
UNROLL = 2


def sincos(x):
    n = jnp.floor(x * two_over_pi + 0.5)
    r = (x - n * 1.5703125) - n * 4.838267923332751e-4
    z = r * r
    s = ((-1.9515295891e-4 * z + 8.3321608736e-3) * z - 1.6666654611e-1) * z * r + r
    c = ((2.443315711809948e-5 * z - 1.388731625493765e-3) * z + 4.166664568298827e-2) * z * z
    c = c - 0.5 * z + 1.0
    q = n.astype(jnp.int32)
    swap = (q & 1) == 1
    s0 = jnp.where(swap, c, s)
    c0 = jnp.where(swap, s, c)
    sin = jnp.where((q & 2) == 2, -s0, s0)
    cos = jnp.where(((q + 1) & 2) == 2, -c0, c0)
    return sin, cos


def green(k, xt, yt, zt, zt4, et, xs, ys, zs, area, sj, cj):
    dx = xt - xs
    dy = yt - ys
    planar = dx * dx + dy * dy
    dz = zt - zs
    near = planar + dz * dz + area
    direct = lax.rsqrt(near)
    mirror = lax.rsqrt(near + zt4 * zs)
    kr = k * jnp.sqrt(planar)
    amp = (et * cj) * lax.rsqrt(1.0 + kr)
    sin, cos = sincos(kr + quarter_turn)
    return sj * (direct + mirror) - amp * sin, amp * cos


def tile_into(k, tb_ref, sb_ref, g, p, tr_ref, ti_ref):
    width = tr_ref.shape[0]
    halves = tr_ref.shape[1] // LANES

    def strip(r, carry):
        rows = pl.ds(pl.multiple_of(r * STRIP, STRIP), STRIP)
        xs = sb_ref[p, 0, rows, :]
        ys = sb_ref[p, 1, rows, :]
        zs = sb_ref[p, 2, rows, :]
        area = sb_ref[p, 3, rows, :]
        sj = sb_ref[p, 4, rows, :]
        cj = sb_ref[p, 5, rows, :]
        for h in range(halves):
            lanes = pl.ds(h * LANES, LANES)
            xt = tb_ref[g, 0, :, lanes]
            yt = tb_ref[g, 1, :, lanes]
            zt = tb_ref[g, 2, :, lanes]
            et = tb_ref[g, 3, :, lanes]
            zt4 = tb_ref[g, 4, :, lanes]
            re, im = green(k, xt, yt, zt, zt4, et, xs, ys, zs, area, sj, cj)
            tr_ref[rows, lanes] = re.astype(jnp.bfloat16)
            ti_ref[rows, lanes] = im.astype(jnp.bfloat16)
        return carry

    lax.fori_loop(0, width // STRIP, strip, 0, unroll=UNROLL)


def entry_product(l_ref, p, tile):
    return jnp.dot(l_ref[p], tile, preferred_element_type=jnp.float32)


def product_kernel(n_ref, g_ref, p_ref, w_ref, k_ref, tb_ref, sb_ref, l_ref, acc_ref, tbuf):
    n = n_ref[0]
    k = k_ref[0]
    acc_ref[...] = jnp.zeros_like(acc_ref)

    def body(e, carry):
        g = g_ref[e]
        p = p_ref[e]
        w = w_ref[e]
        width = tbuf.shape[0] // 2
        tile_into(k, tb_ref, sb_ref, g, p, tbuf.at[pl.ds(0, width)], tbuf.at[pl.ds(width, width)])
        part = entry_product(l_ref, p, tbuf[...])
        acc_ref[g] = acc_ref[g] + w * part
        return carry

    lax.fori_loop(0, n, body, 0)


SMEM_SPEC = pl.BlockSpec(memory_space=pltpu.SMEM)
VMEM_SPEC = pl.BlockSpec(memory_space=pltpu.VMEM)


def product(n, g_list, p_list, w_list, k, tb, sb, lhs):
    clusters = tb.shape[0]
    targets = tb.shape[3]
    nmax = g_list.shape[0]
    width = sb.shape[2]
    cols = lhs.shape[1]
    elems = nmax * width * targets
    return pl.pallas_call(
        product_kernel,
        out_shape=jax.ShapeDtypeStruct((clusters, cols, targets), jnp.float32),
        in_specs=[SMEM_SPEC] * 5 + [VMEM_SPEC] * 3,
        out_specs=VMEM_SPEC,
        scratch_shapes=[pltpu.VMEM((2 * width, targets), jnp.bfloat16)],
        cost_estimate=pl.CostEstimate(
            flops=elems * 60 + 4 * elems * cols,
            transcendentals=elems * 4,
            bytes_accessed=elems * 2,
        ),
    )(n, g_list, p_list, w_list, k, tb, sb, lhs)


def scatter_sum(x, axis):
    count = lax.axis_size(axis)
    if count == 1:
        return x
    me = lax.axis_index(axis)
    blocks = x.reshape((count, x.shape[0] // count) + x.shape[1:])
    total = lax.dynamic_index_in_dim(blocks, me, 0, keepdims=False)
    for shift in range(1, count):
        send = lax.dynamic_index_in_dim(blocks, (me + shift) % count, 0, keepdims=False)
        perm = [(i, (i + shift) % count) for i in range(count)]
        total = total + lax.ppermute(send, axis, perm=perm)
    return total


def local(charges, geometry, wavenumber, requests, pairs, counts):
    clus_index = lax.axis_index("clus")
    src_index = lax.axis_index("src")
    sub_index = lax.axis_index("sub")
    clus_count = lax.axis_size("clus")
    sub_count = lax.axis_size("sub")
    source_rows = charges.shape[0]
    share_rows = source_rows // sub_count
    targets = geometry.shape[2]
    cpd = charges.shape[1]
    wavenum = wavenumber[0]
    slot_total = clus_count * requests.shape[2]

    served = lax.all_to_all(requests[0], "clus", split_axis=0, concat_axis=0, tiled=True).reshape(
        -1
    )
    served_index = jnp.maximum(served, 0)
    served_mask = (served >= 0).astype(jnp.bfloat16)[None, :, None]

    def fetch(values):
        picked = jnp.take(values, served_index, axis=1) * served_mask
        return lax.all_to_all(picked, "clus", split_axis=1, concat_axis=1, tiled=True)

    def lhs_of(values):
        blocks = fetch(values)
        half_width = blocks.shape[2] // 2
        swapped = jnp.concatenate([-blocks[..., half_width:], blocks[..., :half_width]], axis=-1)
        return jnp.concatenate(
            [jnp.transpose(blocks, (1, 2, 0)), jnp.transpose(swapped, (1, 2, 0))], axis=2
        )

    target_geo = lax.dynamic_slice_in_dim(geometry, clus_index * cpd, cpd, axis=1)
    tq = jnp.stack(
        [
            target_geo[0],
            target_geo[1],
            target_geo[2],
            jnp.exp(wavenum * target_geo[2]),
            4.0 * target_geo[2],
        ],
        axis=1,
    )
    tb = jnp.broadcast_to(tq[:, :, None, :], (cpd, tq.shape[1], STRIP, targets))

    base_ids = jnp.arange(clus_count, dtype=jnp.int32)[:, None] * cpd
    source_ids = (base_ids + jnp.maximum(requests[0], 0)).reshape(-1)
    source_full = jnp.take(geometry, source_ids, axis=1)
    source_geo = lax.dynamic_slice_in_dim(source_full, src_index * source_rows, source_rows, axis=2)
    sj = source_geo[3] * inverse_four_pi
    cj = (two_pi * wavenum) * jnp.exp(wavenum * source_geo[2]) * sj
    sq = jnp.stack([source_geo[0], source_geo[1], source_geo[2], source_geo[3], sj, cj], axis=1)
    sb = jnp.broadcast_to(sq[..., None], sq.shape + (LANES,))

    slot_ids = pairs[:, 0, :]
    live = jnp.arange(pairs.shape[2], dtype=jnp.int32)[None, :] < counts[:, 0:1]
    hits = (slot_ids[:, :, None] == jnp.arange(slot_total, dtype=jnp.int32)[None, None, :]) & live[
        :, :, None
    ]
    weight = jnp.sum(hits.astype(jnp.int32), axis=1).reshape(-1)
    nmax = cpd * min(slot_total, pairs.shape[2])
    order = jnp.argsort((weight == 0).astype(jnp.int32), stable=True)[:nmax].astype(jnp.int32)
    g_list = order // slot_total
    p_list = order % slot_total
    w_list = jnp.take(weight, order).astype(jnp.float32)
    n = jnp.sum((weight > 0).astype(jnp.int32)).reshape(1)
    k_arr = wavenumber.astype(jnp.float32).reshape(1)

    src_count = lax.axis_size("src")

    def finish(acc):
        clusters, cols, _ = acc.shape
        rows = targets // (src_count * sub_count)
        split = acc.reshape(clusters, cols, src_count, sub_count, rows)
        ordered = jnp.transpose(split, (3, 2, 4, 0, 1)).reshape(targets, clusters, cols)
        return scatter_sum(scatter_sum(ordered, "sub"), "src")

    first = finish(product(n, g_list, p_list, w_list, k_arr, tb, sb, lhs_of(charges)))
    own_rows = lax.dynamic_slice_in_dim(charges, sub_index * share_rows, share_rows, axis=0)
    iterate_share = (own_rows.astype(jnp.float32) - first).astype(jnp.bfloat16)
    iterate = lax.all_gather(iterate_share, "sub", axis=0, tiled=True)
    image = finish(product(n, g_list, p_list, w_list, k_arr, tb, sb, lhs_of(iterate)))
    return (iterate, image)


def solution(mesh):
    in_specs = (
        P(("freq", "src"), "clus", None),
        P(),
        P("freq"),
        P(("clus", "sub"), None, None),
        P("clus", "sub", None),
        P("clus", "sub"),
    )
    out_specs = (P(("freq", "src"), "clus", None), P(("freq", "src", "sub"), "clus", None))
    return jax.shard_map(local, mesh=mesh, in_specs=in_specs, out_specs=out_specs, check_vma=False)
```

```python
import jax
import jax.numpy as jnp
from jax import lax
from jax.experimental import pallas as pl
from jax.experimental.pallas import tpu as pltpu
from jax.sharding import PartitionSpec as P

CPD = 12
CAP = 4
PPT = 32

quarter_turn = 0.7853981633974483
two_pi = 6.283185307179586
inverse_four_pi = 0.07957747154594767
two_over_pi = 0.6366197723675814

STRIP = 16
LANES = 128
UNROLL = 2


def sincos(x):
    n = jnp.floor(x * two_over_pi + 0.5)
    r = (x - n * 1.5703125) - n * 4.838267923332751e-4
    z = r * r
    s = ((-1.9515295891e-4 * z + 8.3321608736e-3) * z - 1.6666654611e-1) * z * r + r
    c = ((2.443315711809948e-5 * z - 1.388731625493765e-3) * z + 4.166664568298827e-2) * z * z
    c = c - 0.5 * z + 1.0
    q = n.astype(jnp.int32)
    swap = (q & 1) == 1
    s0 = jnp.where(swap, c, s)
    c0 = jnp.where(swap, s, c)
    sin = jnp.where((q & 2) == 2, -s0, s0)
    cos = jnp.where(((q + 1) & 2) == 2, -c0, c0)
    return sin, cos


def green(k, xt, yt, zt, zt4, et, xs, ys, zs, area, sj, cj):
    dx = xt - xs
    dy = yt - ys
    planar = dx * dx + dy * dy
    dz = zt - zs
    near = planar + dz * dz + area
    direct = lax.rsqrt(near)
    mirror = lax.rsqrt(near + zt4 * zs)
    kr = k * jnp.sqrt(planar)
    amp = (et * cj) * lax.rsqrt(1.0 + kr)
    sin, cos = sincos(kr + quarter_turn)
    return sj * (direct + mirror) - amp * sin, amp * cos


def tile_into(k, tb_ref, sb_ref, g, p, tr_ref, ti_ref):
    width = tr_ref.shape[0]
    halves = tr_ref.shape[1] // LANES

    def strip(r, carry):
        rows = pl.ds(pl.multiple_of(r * STRIP, STRIP), STRIP)
        xs = sb_ref[p, 0, rows, :]
        ys = sb_ref[p, 1, rows, :]
        zs = sb_ref[p, 2, rows, :]
        area = sb_ref[p, 3, rows, :]
        sj = sb_ref[p, 4, rows, :]
        cj = sb_ref[p, 5, rows, :]
        for h in range(halves):
            lanes = pl.ds(h * LANES, LANES)
            xt = tb_ref[g, 0, :, lanes]
            yt = tb_ref[g, 1, :, lanes]
            zt = tb_ref[g, 2, :, lanes]
            et = tb_ref[g, 3, :, lanes]
            zt4 = tb_ref[g, 4, :, lanes]
            re, im = green(k, xt, yt, zt, zt4, et, xs, ys, zs, area, sj, cj)
            tr_ref[rows, lanes] = re.astype(jnp.bfloat16)
            ti_ref[rows, lanes] = im.astype(jnp.bfloat16)
        return carry

    lax.fori_loop(0, width // STRIP, strip, 0, unroll=UNROLL)


def entry_product(l_ref, p, tile):
    return jnp.dot(l_ref[p], tile, preferred_element_type=jnp.float32)


def product_kernel(w_ref, k_ref, tb_ref, sb_ref, l_ref, acc_ref, tbuf):
    k = k_ref[0]
    slots = sb_ref.shape[0]
    width = tbuf.shape[0] // 2
    acc_ref[...] = jnp.zeros_like(acc_ref)

    def body(e, carry):
        w = w_ref[e]

        @pl.when(w > 0.0)
        def _():
            g = e // slots
            p = e % slots
            tile_into(k, tb_ref, sb_ref, g, p, tbuf.at[pl.ds(0, width)], tbuf.at[pl.ds(width, width)])
            part = entry_product(l_ref, p, tbuf[...])
            acc_ref[g] = acc_ref[g] + w * part

        return carry

    lax.fori_loop(0, w_ref.shape[0], body, 0)


SMEM_SPEC = pl.BlockSpec(memory_space=pltpu.SMEM)
VMEM_SPEC = pl.BlockSpec(memory_space=pltpu.VMEM)


def product(w_list, k, tb, sb, lhs):
    clusters = tb.shape[0]
    targets = tb.shape[3]
    width = sb.shape[2]
    cols = lhs.shape[1]
    elems = clusters * width * targets * PPT
    return pl.pallas_call(
        product_kernel,
        out_shape=jax.ShapeDtypeStruct((clusters, cols, targets), jnp.float32),
        in_specs=[SMEM_SPEC] * 2 + [VMEM_SPEC] * 3,
        out_specs=VMEM_SPEC,
        scratch_shapes=[pltpu.VMEM((2 * width, targets), jnp.bfloat16)],
        cost_estimate=pl.CostEstimate(
            flops=elems * 60 + 4 * elems * cols,
            transcendentals=elems * 4,
            bytes_accessed=elems * 2,
        ),
    )(w_list, k, tb, sb, lhs)


def scatter_sum(x, axis):
    count = lax.axis_size(axis)
    if count == 1:
        return x
    me = lax.axis_index(axis)
    blocks = x.reshape((count, x.shape[0] // count) + x.shape[1:])
    total = lax.dynamic_index_in_dim(blocks, me, 0, keepdims=False)
    for shift in range(1, count):
        send = lax.dynamic_index_in_dim(blocks, (me + shift) % count, 0, keepdims=False)
        perm = [(i, (i + shift) % count) for i in range(count)]
        total = total + lax.ppermute(send, axis, perm=perm)
    return total


def local(charges, geometry, wavenumber, requests, pairs, counts):
    clus_index = lax.axis_index("clus")
    src_index = lax.axis_index("src")
    sub_index = lax.axis_index("sub")
    clus_count = lax.axis_size("clus")
    sub_count = lax.axis_size("sub")
    source_rows = charges.shape[0]
    share_rows = source_rows // sub_count
    targets = geometry.shape[2]
    cpd = charges.shape[1]
    wavenum = wavenumber[0]
    slot_total = clus_count * requests.shape[2]

    served = lax.all_to_all(requests[0], "clus", split_axis=0, concat_axis=0, tiled=True).reshape(
        -1
    )
    served_index = jnp.maximum(served, 0)
    served_mask = (served >= 0).astype(jnp.bfloat16)[None, :, None]

    def fetch(values):
        picked = jnp.take(values, served_index, axis=1) * served_mask
        return lax.all_to_all(picked, "clus", split_axis=1, concat_axis=1, tiled=True)

    def lhs_of(values):
        blocks = fetch(values)
        half_width = blocks.shape[2] // 2
        swapped = jnp.concatenate([-blocks[..., half_width:], blocks[..., :half_width]], axis=-1)
        return jnp.concatenate(
            [jnp.transpose(blocks, (1, 2, 0)), jnp.transpose(swapped, (1, 2, 0))], axis=2
        )

    target_geo = lax.dynamic_slice_in_dim(geometry, clus_index * cpd, cpd, axis=1)
    tq = jnp.stack(
        [
            target_geo[0],
            target_geo[1],
            target_geo[2],
            jnp.exp(wavenum * target_geo[2]),
            4.0 * target_geo[2],
        ],
        axis=1,
    )
    tb = jnp.broadcast_to(tq[:, :, None, :], (cpd, tq.shape[1], STRIP, targets))

    base_ids = jnp.arange(clus_count, dtype=jnp.int32)[:, None] * cpd
    source_ids = (base_ids + jnp.maximum(requests[0], 0)).reshape(-1)
    source_full = jnp.take(geometry, source_ids, axis=1)
    source_geo = lax.dynamic_slice_in_dim(source_full, src_index * source_rows, source_rows, axis=2)
    sj = source_geo[3] * inverse_four_pi
    cj = (two_pi * wavenum) * jnp.exp(wavenum * source_geo[2]) * sj
    sq = jnp.stack([source_geo[0], source_geo[1], source_geo[2], source_geo[3], sj, cj], axis=1)
    sb = jnp.broadcast_to(sq[..., None], sq.shape + (LANES,))

    slot_ids = pairs[:, 0, :]
    live = jnp.arange(pairs.shape[2], dtype=jnp.int32)[None, :] < counts[:, 0:1]
    hits = (slot_ids[:, :, None] == jnp.arange(slot_total, dtype=jnp.int32)[None, None, :]) & live[
        :, :, None
    ]
    w_list = jnp.sum(hits.astype(jnp.float32), axis=1).reshape(-1)
    k_arr = wavenumber.astype(jnp.float32).reshape(1)

    src_count = lax.axis_size("src")

    def finish(acc):
        clusters, cols, _ = acc.shape
        rows = targets // (src_count * sub_count)
        split = acc.reshape(clusters, cols, src_count, sub_count, rows)
        ordered = jnp.transpose(split, (3, 2, 4, 0, 1)).reshape(targets, clusters, cols)
        return scatter_sum(scatter_sum(ordered, "sub"), "src")

    first = finish(product(w_list, k_arr, tb, sb, lhs_of(charges)))
    own_rows = lax.dynamic_slice_in_dim(charges, sub_index * share_rows, share_rows, axis=0)
    iterate_share = (own_rows.astype(jnp.float32) - first).astype(jnp.bfloat16)
    iterate = lax.all_gather(iterate_share, "sub", axis=0, tiled=True)
    image = finish(product(w_list, k_arr, tb, sb, lhs_of(iterate)))
    return (iterate, image)


def solution(mesh):
    in_specs = (
        P(("freq", "src"), "clus", None),
        P(),
        P("freq"),
        P(("clus", "sub"), None, None),
        P("clus", "sub", None),
        P("clus", "sub"),
    )
    out_specs = (P(("freq", "src"), "clus", None), P(("freq", "src", "sub"), "clus", None))
    return jax.shard_map(local, mesh=mesh, in_specs=in_specs, out_specs=out_specs, check_vma=False)
```

```python
import jax
import jax.numpy as jnp
from jax import lax
from jax.experimental import pallas as pl
from jax.experimental.pallas import tpu as pltpu
from jax.sharding import PartitionSpec as P

CPD = 12
CAP = 4
PPT = 32

quarter_turn = 0.7853981633974483
two_pi = 6.283185307179586
inverse_four_pi = 0.07957747154594767
two_over_pi = 0.6366197723675814

STRIP = 16
LANES = 128
UNROLL = 2


def sincos(x):
    n = jnp.floor(x * two_over_pi + 0.5)
    r = (x - n * 1.5703125) - n * 4.838267923332751e-4
    z = r * r
    s = ((-1.9515295891e-4 * z + 8.3321608736e-3) * z - 1.6666654611e-1) * z * r + r
    c = ((2.443315711809948e-5 * z - 1.388731625493765e-3) * z + 4.166664568298827e-2) * z * z
    c = c - 0.5 * z + 1.0
    q = n.astype(jnp.int32)
    swap = (q & 1) == 1
    s0 = jnp.where(swap, c, s)
    c0 = jnp.where(swap, s, c)
    sin = jnp.where((q & 2) == 2, -s0, s0)
    cos = jnp.where(((q + 1) & 2) == 2, -c0, c0)
    return sin, cos


def green(k, xt, yt, zt, zt4, et, xs, ys, zs, area, sj, cj):
    dx = xt - xs
    dy = yt - ys
    planar = dx * dx + dy * dy
    dz = zt - zs
    near = planar + dz * dz + area
    direct = lax.rsqrt(near)
    mirror = lax.rsqrt(near + zt4 * zs)
    kr = k * jnp.sqrt(planar)
    amp = (et * cj) * lax.rsqrt(1.0 + kr)
    sin, cos = sincos(kr + quarter_turn)
    return sj * (direct + mirror) - amp * sin, amp * cos


def tile_into(k, tb_ref, sb_ref, g, p, tr_ref, ti_ref):
    width = tr_ref.shape[0]
    halves = tr_ref.shape[1] // LANES

    def strip(r, carry):
        rows = pl.ds(pl.multiple_of(r * STRIP, STRIP), STRIP)
        xs = sb_ref[p, 0, rows, :]
        ys = sb_ref[p, 1, rows, :]
        zs = sb_ref[p, 2, rows, :]
        area = sb_ref[p, 3, rows, :]
        sj = sb_ref[p, 4, rows, :]
        cj = sb_ref[p, 5, rows, :]
        for h in range(halves):
            lanes = pl.ds(h * LANES, LANES)
            xt = tb_ref[g, 0, :, lanes]
            yt = tb_ref[g, 1, :, lanes]
            zt = tb_ref[g, 2, :, lanes]
            et = tb_ref[g, 3, :, lanes]
            zt4 = tb_ref[g, 4, :, lanes]
            re, im = green(k, xt, yt, zt, zt4, et, xs, ys, zs, area, sj, cj)
            tr_ref[rows, lanes] = re.astype(jnp.bfloat16)
            ti_ref[rows, lanes] = im.astype(jnp.bfloat16)
        return carry

    lax.fori_loop(0, width // STRIP, strip, 0, unroll=UNROLL)


def entry_product(l_ref, p, tile):
    return jnp.dot(l_ref[p], tile, preferred_element_type=jnp.float32)


def product_kernel(w_ref, k_ref, tb_ref, sb_ref, l_ref, acc_ref, tbuf):
    k = k_ref[0]
    slots = sb_ref.shape[0]
    width = tbuf.shape[0] // 2
    acc_ref[...] = jnp.zeros_like(acc_ref)

    def body(e, carry):
        w = w_ref[e]

        @pl.when(w > 0.0)
        def _():
            g = e // slots
            p = e % slots
            tile_into(k, tb_ref, sb_ref, g, p, tbuf.at[pl.ds(0, width)], tbuf.at[pl.ds(width, width)])
            part = entry_product(l_ref, p, tbuf[...])
            acc_ref[g] = acc_ref[g] + w * part

        return carry

    lax.fori_loop(0, w_ref.shape[0], body, 0)


SMEM_SPEC = pl.BlockSpec(memory_space=pltpu.SMEM)
VMEM_SPEC = pl.BlockSpec(memory_space=pltpu.VMEM)


def product(w_list, k, tb, sb, lhs):
    clusters = tb.shape[0]
    targets = tb.shape[3]
    width = sb.shape[2]
    cols = lhs.shape[1]
    elems = clusters * width * targets * PPT
    return pl.pallas_call(
        product_kernel,
        out_shape=jax.ShapeDtypeStruct((clusters, cols, targets), jnp.float32),
        in_specs=[SMEM_SPEC] * 2 + [VMEM_SPEC] * 3,
        out_specs=VMEM_SPEC,
        scratch_shapes=[pltpu.VMEM((2 * width, targets), jnp.bfloat16)],
        cost_estimate=pl.CostEstimate(
            flops=elems * 60 + 4 * elems * cols,
            transcendentals=elems * 4,
            bytes_accessed=elems * 2,
        ),
    )(w_list, k, tb, sb, lhs)


def scatter_sum(x, axis):
    count = lax.axis_size(axis)
    if count == 1:
        return x
    me = lax.axis_index(axis)
    blocks = x.reshape((count, x.shape[0] // count) + x.shape[1:])
    total = lax.dynamic_index_in_dim(blocks, me, 0, keepdims=False)
    for shift in range(1, count):
        send = lax.dynamic_index_in_dim(blocks, (me + shift) % count, 0, keepdims=False)
        perm = [(i, (i + shift) % count) for i in range(count)]
        total = total + lax.ppermute(send, axis, perm=perm)
    return total


def local(charges, geometry, wavenumber, requests, pairs, counts):
    clus_index = lax.axis_index("clus")
    src_index = lax.axis_index("src")
    sub_index = lax.axis_index("sub")
    clus_count = lax.axis_size("clus")
    sub_count = lax.axis_size("sub")
    source_rows = charges.shape[0]
    share_rows = source_rows // sub_count
    targets = geometry.shape[2]
    cpd = charges.shape[1]
    wavenum = wavenumber[0]
    slot_total = clus_count * requests.shape[2]

    def lhs_of(values_all):
        blocks = jnp.take(values_all, source_ids, axis=1)
        half_width = blocks.shape[2] // 2
        swapped = jnp.concatenate([-blocks[..., half_width:], blocks[..., :half_width]], axis=-1)
        return jnp.concatenate(
            [jnp.transpose(blocks, (1, 2, 0)), jnp.transpose(swapped, (1, 2, 0))], axis=2
        )

    target_geo = lax.dynamic_slice_in_dim(geometry, clus_index * cpd, cpd, axis=1)
    tq = jnp.stack(
        [
            target_geo[0],
            target_geo[1],
            target_geo[2],
            jnp.exp(wavenum * target_geo[2]),
            4.0 * target_geo[2],
        ],
        axis=1,
    )
    tb = jnp.broadcast_to(tq[:, :, None, :], (cpd, tq.shape[1], STRIP, targets))

    base_ids = jnp.arange(clus_count, dtype=jnp.int32)[:, None] * cpd
    source_ids = (base_ids + jnp.maximum(requests[0], 0)).reshape(-1)
    source_full = jnp.take(geometry, source_ids, axis=1)
    source_geo = lax.dynamic_slice_in_dim(source_full, src_index * source_rows, source_rows, axis=2)
    sj = source_geo[3] * inverse_four_pi
    cj = (two_pi * wavenum) * jnp.exp(wavenum * source_geo[2]) * sj
    sq = jnp.stack([source_geo[0], source_geo[1], source_geo[2], source_geo[3], sj, cj], axis=1)
    sb = jnp.broadcast_to(sq[..., None], sq.shape + (LANES,))

    slot_ids = pairs[:, 0, :]
    live = jnp.arange(pairs.shape[2], dtype=jnp.int32)[None, :] < counts[:, 0:1]
    hits = (slot_ids[:, :, None] == jnp.arange(slot_total, dtype=jnp.int32)[None, None, :]) & live[
        :, :, None
    ]
    w_list = jnp.sum(hits.astype(jnp.float32), axis=1).reshape(-1)
    k_arr = wavenumber.astype(jnp.float32).reshape(1)

    src_count = lax.axis_size("src")

    def finish(acc):
        clusters, cols, _ = acc.shape
        rows = targets // (src_count * sub_count)
        split = acc.reshape(clusters, cols, src_count, sub_count, rows)
        ordered = jnp.transpose(split, (3, 2, 4, 0, 1)).reshape(targets, clusters, cols)
        return scatter_sum(scatter_sum(ordered, "sub"), "src")

    charges_all = lax.all_gather(charges, "clus", axis=1, tiled=True)
    first = finish(product(w_list, k_arr, tb, sb, lhs_of(charges_all)))
    own_rows = lax.dynamic_slice_in_dim(charges, sub_index * share_rows, share_rows, axis=0)
    iterate_share = (own_rows.astype(jnp.float32) - first).astype(jnp.bfloat16)
    gathered = lax.all_gather(iterate_share, ("clus", "sub"), axis=0, tiled=False)
    gathered = gathered.reshape((clus_count, sub_count) + iterate_share.shape)
    iterate = lax.dynamic_index_in_dim(gathered, clus_index, 0, keepdims=False).reshape(
        charges.shape
    )
    iterate_all = jnp.transpose(gathered, (1, 2, 0, 3, 4)).reshape(
        (source_rows, clus_count * cpd, charges.shape[2])
    )
    image = finish(product(w_list, k_arr, tb, sb, lhs_of(iterate_all)))
    return (iterate, image)


def solution(mesh):
    in_specs = (
        P(("freq", "src"), "clus", None),
        P(),
        P("freq"),
        P(("clus", "sub"), None, None),
        P("clus", "sub", None),
        P("clus", "sub"),
    )
    out_specs = (P(("freq", "src"), "clus", None), P(("freq", "src", "sub"), "clus", None))
    return jax.shard_map(local, mesh=mesh, in_specs=in_specs, out_specs=out_specs, check_vma=False)
```

```python
import jax
import jax.numpy as jnp
from jax import lax
from jax.experimental import pallas as pl
from jax.experimental.pallas import tpu as pltpu
from jax.sharding import PartitionSpec as P

CPD = 12
CAP = 4
PPT = 32

quarter_turn = 0.7853981633974483
two_pi = 6.283185307179586
inverse_four_pi = 0.07957747154594767
two_over_pi = 0.6366197723675814

STRIP = 16
LANES = 128
UNROLL = 2


def sincos(x):
    n = jnp.floor(x * two_over_pi + 0.5)
    r = (x - n * 1.5703125) - n * 4.838267923332751e-4
    z = r * r
    s = ((-1.9515295891e-4 * z + 8.3321608736e-3) * z - 1.6666654611e-1) * z * r + r
    c = ((2.443315711809948e-5 * z - 1.388731625493765e-3) * z + 4.166664568298827e-2) * z * z
    c = c - 0.5 * z + 1.0
    q = n.astype(jnp.int32)
    swap = (q & 1) == 1
    s0 = jnp.where(swap, c, s)
    c0 = jnp.where(swap, s, c)
    sin = jnp.where((q & 2) == 2, -s0, s0)
    cos = jnp.where(((q + 1) & 2) == 2, -c0, c0)
    return sin, cos


def green(k, xt, yt, zt, zt4, et, xs, ys, zs, area, sj, cj):
    dx = xt - xs
    dy = yt - ys
    planar = dx * dx + dy * dy
    dz = zt - zs
    near = planar + dz * dz + area
    direct = lax.rsqrt(near)
    mirror = lax.rsqrt(near + zt4 * zs)
    kr = k * jnp.sqrt(planar)
    amp = (et * cj) * lax.rsqrt(1.0 + kr)
    sin, cos = sincos(kr + quarter_turn)
    return sj * (direct + mirror) - amp * sin, amp * cos


def tile_into(k, tb_ref, sb_ref, g, p, tr_ref, ti_ref):
    width = tr_ref.shape[0]
    halves = tr_ref.shape[1] // LANES

    def strip(r, carry):
        rows = pl.ds(pl.multiple_of(r * STRIP, STRIP), STRIP)
        xs = sb_ref[p, 0, rows, :]
        ys = sb_ref[p, 1, rows, :]
        zs = sb_ref[p, 2, rows, :]
        area = sb_ref[p, 3, rows, :]
        sj = sb_ref[p, 4, rows, :]
        cj = sb_ref[p, 5, rows, :]
        for h in range(halves):
            lanes = pl.ds(h * LANES, LANES)
            xt = tb_ref[g, 0, :, lanes]
            yt = tb_ref[g, 1, :, lanes]
            zt = tb_ref[g, 2, :, lanes]
            et = tb_ref[g, 3, :, lanes]
            zt4 = tb_ref[g, 4, :, lanes]
            re, im = green(k, xt, yt, zt, zt4, et, xs, ys, zs, area, sj, cj)
            tr_ref[rows, lanes] = re.astype(jnp.bfloat16)
            ti_ref[rows, lanes] = im.astype(jnp.bfloat16)
        return carry

    lax.fori_loop(0, width // STRIP, strip, 0, unroll=UNROLL)


def entry_product(l_ref, p, tile):
    return jnp.dot(l_ref[p], tile, preferred_element_type=jnp.float32)


def product_kernel(w_ref, k_ref, tb_ref, sb_ref, l_ref, acc_ref, tbuf):
    k = k_ref[0]
    slots = sb_ref.shape[0]
    width = tbuf.shape[0] // 2
    acc_ref[...] = jnp.zeros_like(acc_ref)

    def body(e, carry):
        w = w_ref[e]

        @pl.when(w > 0.0)
        def _():
            g = e // slots
            p = e % slots
            tile_into(k, tb_ref, sb_ref, g, p, tbuf.at[pl.ds(0, width)], tbuf.at[pl.ds(width, width)])
            part = entry_product(l_ref, p, tbuf[...])
            acc_ref[g] = acc_ref[g] + w * part

        return carry

    lax.fori_loop(0, w_ref.shape[0], body, 0)


SMEM_SPEC = pl.BlockSpec(memory_space=pltpu.SMEM)
VMEM_SPEC = pl.BlockSpec(memory_space=pltpu.VMEM)


def product(w_list, k, tb, sb, lhs):
    clusters = tb.shape[0]
    targets = tb.shape[3]
    width = sb.shape[2]
    cols = lhs.shape[1]
    elems = clusters * width * targets * PPT
    return pl.pallas_call(
        product_kernel,
        out_shape=jax.ShapeDtypeStruct((clusters, cols, targets), jnp.float32),
        in_specs=[SMEM_SPEC] * 2 + [VMEM_SPEC] * 3,
        out_specs=VMEM_SPEC,
        scratch_shapes=[pltpu.VMEM((2 * width, targets), jnp.bfloat16)],
        cost_estimate=pl.CostEstimate(
            flops=elems * 60 + 4 * elems * cols,
            transcendentals=elems * 4,
            bytes_accessed=elems * 2,
        ),
    )(w_list, k, tb, sb, lhs)


def scatter_sum(x, axis):
    count = lax.axis_size(axis)
    if count == 1:
        return x
    me = lax.axis_index(axis)
    blocks = x.reshape((count, x.shape[0] // count) + x.shape[1:])
    total = lax.dynamic_index_in_dim(blocks, me, 0, keepdims=False)
    for shift in range(1, count):
        send = lax.dynamic_index_in_dim(blocks, (me + shift) % count, 0, keepdims=False)
        perm = [(i, (i + shift) % count) for i in range(count)]
        half = send.shape[0] // 2
        low = lax.ppermute(send[:half], axis, perm=perm)
        high = lax.ppermute(send[half:], axis, perm=perm)
        total = total + jnp.concatenate([low, high], axis=0)
    return total


def local(charges, geometry, wavenumber, requests, pairs, counts):
    clus_index = lax.axis_index("clus")
    src_index = lax.axis_index("src")
    sub_index = lax.axis_index("sub")
    clus_count = lax.axis_size("clus")
    sub_count = lax.axis_size("sub")
    source_rows = charges.shape[0]
    share_rows = source_rows // sub_count
    targets = geometry.shape[2]
    cpd = charges.shape[1]
    wavenum = wavenumber[0]
    slot_total = clus_count * requests.shape[2]

    served = lax.all_to_all(requests[0], "clus", split_axis=0, concat_axis=0, tiled=True).reshape(
        -1
    )
    served_index = jnp.maximum(served, 0)
    served_mask = (served >= 0).astype(jnp.bfloat16)[None, :, None]

    def fetch(values):
        picked = jnp.take(values, served_index, axis=1) * served_mask
        return lax.all_to_all(picked, "clus", split_axis=1, concat_axis=1, tiled=True)

    def lhs_of(values):
        blocks = fetch(values)
        half_width = blocks.shape[2] // 2
        swapped = jnp.concatenate([-blocks[..., half_width:], blocks[..., :half_width]], axis=-1)
        return jnp.concatenate(
            [jnp.transpose(blocks, (1, 2, 0)), jnp.transpose(swapped, (1, 2, 0))], axis=2
        )

    target_geo = lax.dynamic_slice_in_dim(geometry, clus_index * cpd, cpd, axis=1)
    tq = jnp.stack(
        [
            target_geo[0],
            target_geo[1],
            target_geo[2],
            jnp.exp(wavenum * target_geo[2]),
            4.0 * target_geo[2],
        ],
        axis=1,
    )
    tb = jnp.broadcast_to(tq[:, :, None, :], (cpd, tq.shape[1], STRIP, targets))

    base_ids = jnp.arange(clus_count, dtype=jnp.int32)[:, None] * cpd
    source_ids = (base_ids + jnp.maximum(requests[0], 0)).reshape(-1)
    source_full = jnp.take(geometry, source_ids, axis=1)
    source_geo = lax.dynamic_slice_in_dim(source_full, src_index * source_rows, source_rows, axis=2)
    sj = source_geo[3] * inverse_four_pi
    cj = (two_pi * wavenum) * jnp.exp(wavenum * source_geo[2]) * sj
    sq = jnp.stack([source_geo[0], source_geo[1], source_geo[2], source_geo[3], sj, cj], axis=1)
    sb = jnp.broadcast_to(sq[..., None], sq.shape + (LANES,))

    slot_ids = pairs[:, 0, :]
    live = jnp.arange(pairs.shape[2], dtype=jnp.int32)[None, :] < counts[:, 0:1]
    hits = (slot_ids[:, :, None] == jnp.arange(slot_total, dtype=jnp.int32)[None, None, :]) & live[
        :, :, None
    ]
    w_list = jnp.sum(hits.astype(jnp.float32), axis=1).reshape(-1)
    k_arr = wavenumber.astype(jnp.float32).reshape(1)

    src_count = lax.axis_size("src")

    def finish(acc):
        clusters, cols, _ = acc.shape
        rows = targets // (src_count * sub_count)
        split = acc.reshape(clusters, cols, src_count, sub_count, rows)
        ordered = jnp.transpose(split, (3, 2, 4, 0, 1)).reshape(targets, clusters, cols)
        return scatter_sum(scatter_sum(ordered, "sub"), "src")

    first = finish(product(w_list, k_arr, tb, sb, lhs_of(charges)))
    own_rows = lax.dynamic_slice_in_dim(charges, sub_index * share_rows, share_rows, axis=0)
    iterate_share = (own_rows.astype(jnp.float32) - first).astype(jnp.bfloat16)
    iterate = lax.all_gather(iterate_share, "sub", axis=0, tiled=True)
    image = finish(product(w_list, k_arr, tb, sb, lhs_of(iterate)))
    return (iterate, image)


def solution(mesh):
    in_specs = (
        P(("freq", "src"), "clus", None),
        P(),
        P("freq"),
        P(("clus", "sub"), None, None),
        P("clus", "sub", None),
        P("clus", "sub"),
    )
    out_specs = (P(("freq", "src"), "clus", None), P(("freq", "src", "sub"), "clus", None))
    return jax.shard_map(local, mesh=mesh, in_specs=in_specs, out_specs=out_specs, check_vma=False)
```

```python
import jax
import jax.numpy as jnp
from jax import lax
from jax.experimental import pallas as pl
from jax.experimental.pallas import tpu as pltpu
from jax.sharding import PartitionSpec as P

CPD = 12
CAP = 4
PPT = 32

quarter_turn = 0.7853981633974483
two_pi = 6.283185307179586
inverse_four_pi = 0.07957747154594767
inverse_pi = 0.3183098861837907
SIN_A = (-0.16666661577130884, 0.008333118573140752, -0.00019813475437141734, 2.6144256303410747e-06)
COS_B = (
    -0.4999999981796688,
    0.041666651863571776,
    -0.0013888547499597086,
    2.4769209821955003e-05,
    -2.620509973872218e-07,
)

STRIP = 16
LANES = 128
UNROLL = 4


def green(k, xt, yt, zt, zt4, et, xs, ys, zs, area, sj, cj):
    dx = xt - xs
    dy = yt - ys
    planar = dx * dx + dy * dy
    dz = zt - zs
    near = planar + dz * dz + area
    direct = lax.rsqrt(near)
    mirror = lax.rsqrt(near + zt4 * zs)
    kr = k * (planar * lax.rsqrt(jnp.maximum(planar, 1e-30)))
    amp = (et * cj) * lax.rsqrt(1.0 + kr)
    phase = kr + quarter_turn
    n = jnp.floor(phase * inverse_pi + 0.5)
    r = (phase - n * 3.140625) - n * 0.0009676535846665502
    z = r * r
    sin = r + r * (z * (SIN_A[0] + z * (SIN_A[1] + z * (SIN_A[2] + z * SIN_A[3]))))
    cos = 1.0 + z * (COS_B[0] + z * (COS_B[1] + z * (COS_B[2] + z * (COS_B[3] + z * COS_B[4]))))
    amp = jnp.where((n.astype(jnp.int32) & 1) == 1, -amp, amp)
    return sj * (direct + mirror) - amp * sin, amp * cos


def tile_into(k, tb_ref, sb_ref, g, p, tr_ref, ti_ref):
    width = tr_ref.shape[0]
    halves = tr_ref.shape[1] // LANES

    def strip(r, carry):
        rows = pl.ds(pl.multiple_of(r * STRIP, STRIP), STRIP)
        xs = sb_ref[p, 0, rows, :]
        ys = sb_ref[p, 1, rows, :]
        zs = sb_ref[p, 2, rows, :]
        area = sb_ref[p, 3, rows, :]
        sj = sb_ref[p, 4, rows, :]
        cj = sb_ref[p, 5, rows, :]
        for h in range(halves):
            lanes = pl.ds(h * LANES, LANES)
            xt = tb_ref[g, 0, :, lanes]
            yt = tb_ref[g, 1, :, lanes]
            zt = tb_ref[g, 2, :, lanes]
            et = tb_ref[g, 3, :, lanes]
            zt4 = tb_ref[g, 4, :, lanes]
            re, im = green(k, xt, yt, zt, zt4, et, xs, ys, zs, area, sj, cj)
            tr_ref[rows, lanes] = re.astype(jnp.bfloat16)
            ti_ref[rows, lanes] = im.astype(jnp.bfloat16)
        return carry

    lax.fori_loop(0, width // STRIP, strip, 0, unroll=UNROLL)


def entry_product(l_ref, p, tile):
    return jnp.dot(l_ref[p], tile, preferred_element_type=jnp.float32)


def product_kernel(w_ref, k_ref, tb_ref, sb_ref, l_ref, acc_ref, tbuf):
    k = k_ref[0]
    slots = sb_ref.shape[0]
    width = tbuf.shape[0] // 2
    acc_ref[...] = jnp.zeros_like(acc_ref)

    def body(e, carry):
        w = w_ref[e]

        @pl.when(w > 0.0)
        def _():
            g = e // slots
            p = e % slots
            tile_into(k, tb_ref, sb_ref, g, p, tbuf.at[pl.ds(0, width)], tbuf.at[pl.ds(width, width)])
            part = entry_product(l_ref, p, tbuf[...])
            acc_ref[g] = acc_ref[g] + w * part

        return carry

    lax.fori_loop(0, w_ref.shape[0], body, 0)


SMEM_SPEC = pl.BlockSpec(memory_space=pltpu.SMEM)
VMEM_SPEC = pl.BlockSpec(memory_space=pltpu.VMEM)


def product(w_list, k, tb, sb, lhs):
    clusters = tb.shape[0]
    targets = tb.shape[3]
    width = sb.shape[2]
    cols = lhs.shape[1]
    elems = clusters * width * targets * PPT
    return pl.pallas_call(
        product_kernel,
        out_shape=jax.ShapeDtypeStruct((clusters, cols, targets), jnp.float32),
        in_specs=[SMEM_SPEC] * 2 + [VMEM_SPEC] * 3,
        out_specs=VMEM_SPEC,
        scratch_shapes=[pltpu.VMEM((2 * width, targets), jnp.bfloat16)],
        cost_estimate=pl.CostEstimate(
            flops=elems * 60 + 4 * elems * cols,
            transcendentals=elems * 4,
            bytes_accessed=elems * 2,
        ),
    )(w_list, k, tb, sb, lhs)


def scatter_sum(x, axis):
    count = lax.axis_size(axis)
    if count == 1:
        return x
    me = lax.axis_index(axis)
    blocks = x.reshape((count, x.shape[0] // count) + x.shape[1:])
    total = lax.dynamic_index_in_dim(blocks, me, 0, keepdims=False)
    for shift in range(1, count):
        send = lax.dynamic_index_in_dim(blocks, (me + shift) % count, 0, keepdims=False)
        perm = [(i, (i + shift) % count) for i in range(count)]
        total = total + lax.ppermute(send, axis, perm=perm)
    return total


def local(charges, geometry, wavenumber, requests, pairs, counts):
    clus_index = lax.axis_index("clus")
    src_index = lax.axis_index("src")
    sub_index = lax.axis_index("sub")
    clus_count = lax.axis_size("clus")
    sub_count = lax.axis_size("sub")
    source_rows = charges.shape[0]
    share_rows = source_rows // sub_count
    targets = geometry.shape[2]
    cpd = charges.shape[1]
    wavenum = wavenumber[0]
    slot_total = clus_count * requests.shape[2]

    served = lax.all_to_all(requests[0], "clus", split_axis=0, concat_axis=0, tiled=True).reshape(
        -1
    )
    served_index = jnp.maximum(served, 0)
    served_mask = (served >= 0).astype(jnp.bfloat16)[None, :, None]

    def fetch(values):
        picked = jnp.take(values, served_index, axis=1) * served_mask
        return lax.all_to_all(picked, "clus", split_axis=1, concat_axis=1, tiled=True)

    def lhs_of(values):
        blocks = fetch(values)
        half_width = blocks.shape[2] // 2
        swapped = jnp.concatenate([-blocks[..., half_width:], blocks[..., :half_width]], axis=-1)
        return jnp.concatenate(
            [jnp.transpose(blocks, (1, 2, 0)), jnp.transpose(swapped, (1, 2, 0))], axis=2
        )

    target_geo = lax.dynamic_slice_in_dim(geometry, clus_index * cpd, cpd, axis=1)
    tq = jnp.stack(
        [
            target_geo[0],
            target_geo[1],
            target_geo[2],
            jnp.exp(wavenum * target_geo[2]),
            4.0 * target_geo[2],
        ],
        axis=1,
    )
    tb = jnp.broadcast_to(tq[:, :, None, :], (cpd, tq.shape[1], STRIP, targets))

    base_ids = jnp.arange(clus_count, dtype=jnp.int32)[:, None] * cpd
    source_ids = (base_ids + jnp.maximum(requests[0], 0)).reshape(-1)
    source_full = jnp.take(geometry, source_ids, axis=1)
    source_geo = lax.dynamic_slice_in_dim(source_full, src_index * source_rows, source_rows, axis=2)
    sj = source_geo[3] * inverse_four_pi
    cj = (two_pi * wavenum) * jnp.exp(wavenum * source_geo[2]) * sj
    sq = jnp.stack([source_geo[0], source_geo[1], source_geo[2], source_geo[3], sj, cj], axis=1)
    sb = jnp.broadcast_to(sq[..., None], sq.shape + (LANES,))

    slot_ids = pairs[:, 0, :]
    live = jnp.arange(pairs.shape[2], dtype=jnp.int32)[None, :] < counts[:, 0:1]
    hits = (slot_ids[:, :, None] == jnp.arange(slot_total, dtype=jnp.int32)[None, None, :]) & live[
        :, :, None
    ]
    w_list = jnp.sum(hits.astype(jnp.float32), axis=1).reshape(-1)
    k_arr = wavenumber.astype(jnp.float32).reshape(1)

    src_count = lax.axis_size("src")

    def finish(acc):
        clusters, cols, _ = acc.shape
        rows = targets // (src_count * sub_count)
        split = acc.reshape(clusters, cols, src_count, sub_count, rows)
        ordered = jnp.transpose(split, (3, 2, 4, 0, 1)).reshape(targets, clusters, cols)
        return scatter_sum(scatter_sum(ordered, "sub"), "src")

    first = finish(product(w_list, k_arr, tb, sb, lhs_of(charges)))
    own_rows = lax.dynamic_slice_in_dim(charges, sub_index * share_rows, share_rows, axis=0)
    iterate_share = (own_rows.astype(jnp.float32) - first).astype(jnp.bfloat16)
    iterate = lax.all_gather(iterate_share, "sub", axis=0, tiled=True)
    image = finish(product(w_list, k_arr, tb, sb, lhs_of(iterate)))
    return (iterate, image)


def solution(mesh):
    in_specs = (
        P(("freq", "src"), "clus", None),
        P(),
        P("freq"),
        P(("clus", "sub"), None, None),
        P("clus", "sub", None),
        P("clus", "sub"),
    )
    out_specs = (P(("freq", "src"), "clus", None), P(("freq", "src", "sub"), "clus", None))
    return jax.shard_map(local, mesh=mesh, in_specs=in_specs, out_specs=out_specs, check_vma=False)
```

```python
import functools

import jax
import jax.numpy as jnp
from jax import lax
from jax.experimental import pallas as pl
from jax.experimental.pallas import tpu as pltpu
from jax.sharding import PartitionSpec as P

CPD = 12
CAP = 4
PPT = 32

quarter_turn = 0.7853981633974483
two_pi = 6.283185307179586
inverse_four_pi = 0.07957747154594767
inverse_pi = 0.3183098861837907
SIN_A = (-0.16666661577130884, 0.008333118573140752, -0.00019813475437141734, 2.6144256303410747e-06)
COS_B = (
    -0.4999999981796688,
    0.041666651863571776,
    -0.0013888547499597086,
    2.4769209821955003e-05,
    -2.620509973872218e-07,
)

STRIP = 16
LANES = 128
UNROLL = 4


def green(k, xt, yt, zt, zt4, et, xs, ys, zs, area, sj, cj):
    dx = xt - xs
    dy = yt - ys
    planar = dx * dx + dy * dy
    dz = zt - zs
    near = planar + dz * dz + area
    direct = lax.rsqrt(near)
    mirror = lax.rsqrt(near + zt4 * zs)
    kr = k * (planar * lax.rsqrt(jnp.maximum(planar, 1e-30)))
    amp = (et * cj) * lax.rsqrt(1.0 + kr)
    phase = kr + quarter_turn
    n = jnp.floor(phase * inverse_pi + 0.5)
    r = (phase - n * 3.140625) - n * 0.0009676535846665502
    z = r * r
    sin = r + r * (z * (SIN_A[0] + z * (SIN_A[1] + z * (SIN_A[2] + z * SIN_A[3]))))
    cos = 1.0 + z * (COS_B[0] + z * (COS_B[1] + z * (COS_B[2] + z * (COS_B[3] + z * COS_B[4]))))
    amp = jnp.where((n.astype(jnp.int32) & 1) == 1, -amp, amp)
    return sj * (direct + mirror) - amp * sin, amp * cos


def tile_into(k, tb_ref, sb_ref, g, p, tr_ref, ti_ref):
    width = tr_ref.shape[0]
    halves = tr_ref.shape[1] // LANES

    def strip(r, carry):
        rows = pl.ds(pl.multiple_of(r * STRIP, STRIP), STRIP)
        xs = sb_ref[p, 0, rows, :]
        ys = sb_ref[p, 1, rows, :]
        zs = sb_ref[p, 2, rows, :]
        area = sb_ref[p, 3, rows, :]
        sj = sb_ref[p, 4, rows, :]
        cj = sb_ref[p, 5, rows, :]
        for h in range(halves):
            lanes = pl.ds(h * LANES, LANES)
            xt = tb_ref[g, 0, :, lanes]
            yt = tb_ref[g, 1, :, lanes]
            zt = tb_ref[g, 2, :, lanes]
            et = tb_ref[g, 3, :, lanes]
            zt4 = tb_ref[g, 4, :, lanes]
            re, im = green(k, xt, yt, zt, zt4, et, xs, ys, zs, area, sj, cj)
            tr_ref[rows, lanes] = re.astype(jnp.bfloat16)
            ti_ref[rows, lanes] = im.astype(jnp.bfloat16)
        return carry

    lax.fori_loop(0, width // STRIP, strip, 0, unroll=UNROLL)


def entry_product(l_ref, p, tile):
    return jnp.dot(l_ref[p], tile, preferred_element_type=jnp.float32)


def product_kernel(slots, n_ref, w_ref, k_ref, tb_ref, sb_ref, l_ref, acc_ref, tbuf):
    k = k_ref[0]
    clusters = acc_ref.shape[0]
    width = tbuf.shape[0] // 2
    acc_ref[...] = jnp.zeros_like(acc_ref)

    def body(e, carry):
        w = w_ref[e]

        @pl.when(w > 0.0)
        def _():
            half = e // (clusters * slots)
            g = (e // slots) % clusters
            p = half * slots + e % slots
            tile_into(k, tb_ref, sb_ref, g, p, tbuf.at[pl.ds(0, width)], tbuf.at[pl.ds(width, width)])
            part = entry_product(l_ref, p, tbuf[...])
            acc_ref[g] = acc_ref[g] + w * part

        return carry

    lax.fori_loop(n_ref[0], n_ref[1], body, 0)


SMEM_SPEC = pl.BlockSpec(memory_space=pltpu.SMEM)
VMEM_SPEC = pl.BlockSpec(memory_space=pltpu.VMEM)


def product(n, w_list, k, tb, sb, lhs, slots):
    clusters = tb.shape[0]
    targets = tb.shape[3]
    width = sb.shape[2]
    cols = lhs.shape[1]
    elems = clusters * width * targets * PPT
    return pl.pallas_call(
        functools.partial(product_kernel, slots),
        out_shape=jax.ShapeDtypeStruct((clusters, cols, targets), jnp.float32),
        in_specs=[SMEM_SPEC] * 3 + [VMEM_SPEC] * 3,
        out_specs=VMEM_SPEC,
        scratch_shapes=[pltpu.VMEM((2 * width, targets), jnp.bfloat16)],
        cost_estimate=pl.CostEstimate(
            flops=elems * 60 + 4 * elems * cols,
            transcendentals=elems * 4,
            bytes_accessed=elems * 2,
        ),
    )(n, w_list, k, tb, sb, lhs)


def exchange_all(x, axis):
    count = lax.axis_size(axis)
    if count == 1:
        return x[None]
    me = lax.axis_index(axis)
    by_shift = [x]
    for shift in range(1, count):
        perm = [(i, (i + shift) % count) for i in range(count)]
        by_shift.append(lax.ppermute(x, axis, perm=perm))
    stacked = jnp.stack(by_shift)
    return jnp.take(stacked, (me - jnp.arange(count)) % count, axis=0)


def scatter_sum(x, axis):
    count = lax.axis_size(axis)
    if count == 1:
        return x
    me = lax.axis_index(axis)
    blocks = x.reshape((count, x.shape[0] // count) + x.shape[1:])
    total = lax.dynamic_index_in_dim(blocks, me, 0, keepdims=False)
    for shift in range(1, count):
        send = lax.dynamic_index_in_dim(blocks, (me + shift) % count, 0, keepdims=False)
        perm = [(i, (i + shift) % count) for i in range(count)]
        total = total + lax.ppermute(send, axis, perm=perm)
    return total


def local(charges, geometry, wavenumber, requests, pairs, counts):
    clus_index = lax.axis_index("clus")
    src_index = lax.axis_index("src")
    sub_index = lax.axis_index("sub")
    clus_count = lax.axis_size("clus")
    sub_count = lax.axis_size("sub")
    source_rows = charges.shape[0]
    share_rows = source_rows // sub_count
    targets = geometry.shape[2]
    cpd = charges.shape[1]
    wavenum = wavenumber[0]
    slot_total = clus_count * requests.shape[2]

    served = lax.all_to_all(requests[0], "clus", split_axis=0, concat_axis=0, tiled=True).reshape(
        -1
    )
    served_index = jnp.maximum(served, 0)
    served_mask = (served >= 0).astype(jnp.bfloat16)[None, :, None]

    def fetch(values):
        picked = jnp.take(values, served_index, axis=1) * served_mask
        return lax.all_to_all(picked, "clus", split_axis=1, concat_axis=1, tiled=True)

    def lhs_of(values):
        both = exchange_all(fetch(values), "sub")
        blocks = jnp.concatenate(list(both), axis=1)
        half_width = blocks.shape[2] // 2
        swapped = jnp.concatenate([-blocks[..., half_width:], blocks[..., :half_width]], axis=-1)
        return jnp.concatenate(
            [jnp.transpose(blocks, (1, 2, 0)), jnp.transpose(swapped, (1, 2, 0))], axis=2
        )

    target_geo = lax.dynamic_slice_in_dim(geometry, clus_index * cpd, cpd, axis=1)
    tq = jnp.stack(
        [
            target_geo[0],
            target_geo[1],
            target_geo[2],
            jnp.exp(wavenum * target_geo[2]),
            4.0 * target_geo[2],
        ],
        axis=1,
    )
    tb = jnp.broadcast_to(tq[:, :, None, :], (cpd, tq.shape[1], STRIP, targets))

    slot_ids = pairs[:, 0, :]
    live = jnp.arange(pairs.shape[2], dtype=jnp.int32)[None, :] < counts[:, 0:1]
    hits = (slot_ids[:, :, None] == jnp.arange(slot_total, dtype=jnp.int32)[None, None, :]) & live[
        :, :, None
    ]
    weight = jnp.sum(hits.astype(jnp.int32), axis=1).reshape(-1)

    request_count = requests[0].size
    tables = exchange_all(jnp.concatenate([requests[0].reshape(-1), weight]), "sub")
    requests_all = tables[:, :request_count].reshape((sub_count,) + requests[0].shape)
    w_list = tables[:, request_count:].reshape(-1).astype(jnp.float32)

    base_ids = jnp.arange(clus_count, dtype=jnp.int32)[None, :, None] * cpd
    source_ids = (base_ids + jnp.maximum(requests_all, 0)).reshape(-1)
    source_full = jnp.take(geometry, source_ids, axis=1)
    source_geo = lax.dynamic_slice_in_dim(source_full, src_index * source_rows, source_rows, axis=2)
    sj = source_geo[3] * inverse_four_pi
    cj = (two_pi * wavenum) * jnp.exp(wavenum * source_geo[2]) * sj
    sq = jnp.stack([source_geo[0], source_geo[1], source_geo[2], source_geo[3], sj, cj], axis=1)
    sb = jnp.broadcast_to(sq[..., None], sq.shape + (LANES,))

    rank = jnp.cumsum((w_list > 0).astype(jnp.int32))
    share = (rank[-1] + sub_count - 1) // sub_count
    begin = jnp.sum((rank <= sub_index * share).astype(jnp.int32))
    end = jnp.sum((rank <= (sub_index + 1) * share).astype(jnp.int32))
    n = jnp.stack([begin, end]).astype(jnp.int32)
    k_arr = wavenumber.astype(jnp.float32).reshape(1)

    src_count = lax.axis_size("src")

    def finish(acc):
        clusters, cols, _ = acc.shape
        rows = targets // (src_count * sub_count)
        split = acc.reshape(clusters, cols, src_count, sub_count, rows)
        ordered = jnp.transpose(split, (3, 2, 4, 0, 1)).reshape(targets, clusters, cols)
        return scatter_sum(scatter_sum(ordered, "sub"), "src")

    first = finish(product(n, w_list, k_arr, tb, sb, lhs_of(charges), slot_total))
    own_rows = lax.dynamic_slice_in_dim(charges, sub_index * share_rows, share_rows, axis=0)
    iterate_share = (own_rows.astype(jnp.float32) - first).astype(jnp.bfloat16)
    iterate = lax.all_gather(iterate_share, "sub", axis=0, tiled=True)
    image = finish(product(n, w_list, k_arr, tb, sb, lhs_of(iterate), slot_total))
    return (iterate, image)


def solution(mesh):
    in_specs = (
        P(("freq", "src"), "clus", None),
        P(),
        P("freq"),
        P(("clus", "sub"), None, None),
        P("clus", "sub", None),
        P("clus", "sub"),
    )
    out_specs = (P(("freq", "src"), "clus", None), P(("freq", "src", "sub"), "clus", None))
    return jax.shard_map(local, mesh=mesh, in_specs=in_specs, out_specs=out_specs, check_vma=False)
```

```python
import jax
import jax.numpy as jnp
from jax import lax
from jax.experimental import pallas as pl
from jax.experimental.pallas import tpu as pltpu
from jax.sharding import PartitionSpec as P

CPD = 12
CAP = 4
PPT = 32

quarter_turn = 0.7853981633974483
two_pi = 6.283185307179586
inverse_four_pi = 0.07957747154594767
inverse_pi = 0.3183098861837907
SIN_A = (-0.16666661577130884, 0.008333118573140752, -0.00019813475437141734, 2.6144256303410747e-06)
COS_B = (
    -0.4999999981796688,
    0.041666651863571776,
    -0.0013888547499597086,
    2.4769209821955003e-05,
    -2.620509973872218e-07,
)

STRIP = 16
LANES = 128
UNROLL = 4


def green(k, xt, yt, zt, zt4, et, xs, ys, zs, area, sj, cj):
    dx = xt - xs
    dy = yt - ys
    planar = dx * dx + dy * dy
    dz = zt - zs
    near = planar + dz * dz + area
    direct = lax.rsqrt(near)
    mirror = lax.rsqrt(near + zt4 * zs)
    kr = k * (planar * lax.rsqrt(jnp.maximum(planar, 1e-30)))
    amp = (et * cj) * lax.rsqrt(1.0 + kr)
    phase = kr + quarter_turn
    n = jnp.floor(phase * inverse_pi + 0.5)
    r = (phase - n * 3.140625) - n * 0.0009676535846665502
    z = r * r
    sin = r + r * (z * (SIN_A[0] + z * (SIN_A[1] + z * (SIN_A[2] + z * SIN_A[3]))))
    cos = 1.0 + z * (COS_B[0] + z * (COS_B[1] + z * (COS_B[2] + z * (COS_B[3] + z * COS_B[4]))))
    amp = jnp.where((n.astype(jnp.int32) & 1) == 1, -amp, amp)
    return sj * (direct + mirror) - amp * sin, amp * cos


def tile_into(k, tb_ref, sb_ref, g, p, tr_ref, ti_ref):
    width = tr_ref.shape[0]
    halves = tr_ref.shape[1] // LANES

    def strip(r, carry):
        rows = pl.ds(pl.multiple_of(r * STRIP, STRIP), STRIP)
        xs = sb_ref[p, 0, rows, :]
        ys = sb_ref[p, 1, rows, :]
        zs = sb_ref[p, 2, rows, :]
        area = sb_ref[p, 3, rows, :]
        sj = sb_ref[p, 4, rows, :]
        cj = sb_ref[p, 5, rows, :]
        for h in range(halves):
            lanes = pl.ds(h * LANES, LANES)
            xt = tb_ref[g, 0, :, lanes]
            yt = tb_ref[g, 1, :, lanes]
            zt = tb_ref[g, 2, :, lanes]
            et = tb_ref[g, 3, :, lanes]
            zt4 = tb_ref[g, 4, :, lanes]
            re, im = green(k, xt, yt, zt, zt4, et, xs, ys, zs, area, sj, cj)
            tr_ref[rows, lanes] = re.astype(jnp.bfloat16)
            ti_ref[rows, lanes] = im.astype(jnp.bfloat16)
        return carry

    lax.fori_loop(0, width // STRIP, strip, 0, unroll=UNROLL)


def entry_product(l_ref, p, tile):
    return jnp.dot(l_ref[p], tile, preferred_element_type=jnp.float32)


def product_kernel(w_ref, k_ref, tb_ref, sb_ref, l_ref, acc_ref, tbuf):
    k = k_ref[0]
    slots = sb_ref.shape[0]
    width = tbuf.shape[0] // 2
    acc_ref[...] = jnp.zeros_like(acc_ref)

    def body(e, carry):
        w = w_ref[e]

        @pl.when(w > 0.0)
        def _():
            g = e // slots
            p = e % slots
            tile_into(k, tb_ref, sb_ref, g, p, tbuf.at[pl.ds(0, width)], tbuf.at[pl.ds(width, width)])
            part = entry_product(l_ref, p, tbuf[...])
            acc_ref[g] = acc_ref[g] + w * part

        return carry

    lax.fori_loop(0, w_ref.shape[0], body, 0)


SMEM_SPEC = pl.BlockSpec(memory_space=pltpu.SMEM)
VMEM_SPEC = pl.BlockSpec(memory_space=pltpu.VMEM)


def product(w_list, k, tb, sb, lhs):
    clusters = tb.shape[0]
    targets = tb.shape[3]
    width = sb.shape[2]
    cols = lhs.shape[1]
    elems = clusters * width * targets * PPT
    return pl.pallas_call(
        product_kernel,
        out_shape=jax.ShapeDtypeStruct((clusters, cols, targets), jnp.float32),
        in_specs=[SMEM_SPEC] * 2 + [VMEM_SPEC] * 3,
        out_specs=VMEM_SPEC,
        scratch_shapes=[pltpu.VMEM((2 * width, targets), jnp.bfloat16)],
        cost_estimate=pl.CostEstimate(
            flops=elems * 60 + 4 * elems * cols,
            transcendentals=elems * 4,
            bytes_accessed=elems * 2,
        ),
    )(w_list, k, tb, sb, lhs)


def scatter_sum(x, axis):
    count = lax.axis_size(axis)
    if count == 1:
        return x
    me = lax.axis_index(axis)
    blocks = x.reshape((count, x.shape[0] // count) + x.shape[1:])
    total = lax.dynamic_index_in_dim(blocks, me, 0, keepdims=False)
    for shift in range(1, count):
        send = lax.dynamic_index_in_dim(blocks, (me + shift) % count, 0, keepdims=False)
        perm = [(i, (i + shift) % count) for i in range(count)]
        total = total + lax.ppermute(send, axis, perm=perm)
    return total


def local(charges, geometry, wavenumber, requests, pairs, counts):
    clus_index = lax.axis_index("clus")
    src_index = lax.axis_index("src")
    sub_index = lax.axis_index("sub")
    clus_count = lax.axis_size("clus")
    sub_count = lax.axis_size("sub")
    source_rows = charges.shape[0]
    share_rows = source_rows // sub_count
    targets = geometry.shape[2]
    cpd = charges.shape[1]
    wavenum = wavenumber[0]
    slot_total = clus_count * requests.shape[2]

    served = lax.all_to_all(requests[0], "clus", split_axis=0, concat_axis=0, tiled=True).reshape(
        -1
    )
    served_index = jnp.maximum(served, 0)
    served_mask = (served >= 0).astype(jnp.bfloat16)[None, :, None]

    def fetch(values):
        picked = jnp.take(values, served_index, axis=1) * served_mask
        chunks = picked.reshape(
            (picked.shape[0], clus_count, picked.shape[1] // clus_count) + picked.shape[2:]
        )
        by_shift = [lax.dynamic_index_in_dim(chunks, clus_index, 1, keepdims=False)]
        for shift in range(1, clus_count):
            send = lax.dynamic_index_in_dim(chunks, (clus_index + shift) % clus_count, 1, False)
            perm = [(i, (i + shift) % clus_count) for i in range(clus_count)]
            by_shift.append(lax.ppermute(send, "clus", perm=perm))
        stacked = jnp.stack(by_shift, axis=1)
        ordered = jnp.take(stacked, (clus_index - jnp.arange(clus_count)) % clus_count, axis=1)
        return ordered.reshape(picked.shape)

    def lhs_of(values):
        blocks = fetch(values)
        half_width = blocks.shape[2] // 2
        swapped = jnp.concatenate([-blocks[..., half_width:], blocks[..., :half_width]], axis=-1)
        return jnp.concatenate(
            [jnp.transpose(blocks, (1, 2, 0)), jnp.transpose(swapped, (1, 2, 0))], axis=2
        )

    target_geo = lax.dynamic_slice_in_dim(geometry, clus_index * cpd, cpd, axis=1)
    tq = jnp.stack(
        [
            target_geo[0],
            target_geo[1],
            target_geo[2],
            jnp.exp(wavenum * target_geo[2]),
            4.0 * target_geo[2],
        ],
        axis=1,
    )
    tb = jnp.broadcast_to(tq[:, :, None, :], (cpd, tq.shape[1], STRIP, targets))

    base_ids = jnp.arange(clus_count, dtype=jnp.int32)[:, None] * cpd
    source_ids = (base_ids + jnp.maximum(requests[0], 0)).reshape(-1)
    source_full = jnp.take(geometry, source_ids, axis=1)
    source_geo = lax.dynamic_slice_in_dim(source_full, src_index * source_rows, source_rows, axis=2)
    sj = source_geo[3] * inverse_four_pi
    cj = (two_pi * wavenum) * jnp.exp(wavenum * source_geo[2]) * sj
    sq = jnp.stack([source_geo[0], source_geo[1], source_geo[2], source_geo[3], sj, cj], axis=1)
    sb = jnp.broadcast_to(sq[..., None], sq.shape + (LANES,))

    slot_ids = pairs[:, 0, :]
    live = jnp.arange(pairs.shape[2], dtype=jnp.int32)[None, :] < counts[:, 0:1]
    hits = (slot_ids[:, :, None] == jnp.arange(slot_total, dtype=jnp.int32)[None, None, :]) & live[
        :, :, None
    ]
    w_list = jnp.sum(hits.astype(jnp.float32), axis=1).reshape(-1)
    k_arr = wavenumber.astype(jnp.float32).reshape(1)

    src_count = lax.axis_size("src")

    def finish(acc):
        clusters, cols, _ = acc.shape
        rows = targets // (src_count * sub_count)
        split = acc.reshape(clusters, cols, src_count, sub_count, rows)
        ordered = jnp.transpose(split, (3, 2, 4, 0, 1)).reshape(targets, clusters, cols)
        return scatter_sum(scatter_sum(ordered, "sub"), "src")

    first = finish(product(w_list, k_arr, tb, sb, lhs_of(charges)))
    own_rows = lax.dynamic_slice_in_dim(charges, sub_index * share_rows, share_rows, axis=0)
    iterate_share = (own_rows.astype(jnp.float32) - first).astype(jnp.bfloat16)
    iterate = lax.all_gather(iterate_share, "sub", axis=0, tiled=True)
    image = finish(product(w_list, k_arr, tb, sb, lhs_of(iterate)))
    return (iterate, image)


def solution(mesh):
    in_specs = (
        P(("freq", "src"), "clus", None),
        P(),
        P("freq"),
        P(("clus", "sub"), None, None),
        P("clus", "sub", None),
        P("clus", "sub"),
    )
    out_specs = (P(("freq", "src"), "clus", None), P(("freq", "src", "sub"), "clus", None))
    return jax.shard_map(local, mesh=mesh, in_specs=in_specs, out_specs=out_specs, check_vma=False)
```

```python
import jax
import jax.numpy as jnp
from jax import lax
from jax.experimental import pallas as pl
from jax.experimental.pallas import tpu as pltpu
from jax.sharding import PartitionSpec as P

CPD = 12
CAP = 4
PPT = 32

quarter_turn = 0.7853981633974483
two_pi = 6.283185307179586
inverse_four_pi = 0.07957747154594767
inverse_pi = 0.3183098861837907
SIN_A = (-0.16666661577130884, 0.008333118573140752, -0.00019813475437141734, 2.6144256303410747e-06)
COS_B = (
    -0.4999999981796688,
    0.041666651863571776,
    -0.0013888547499597086,
    2.4769209821955003e-05,
    -2.620509973872218e-07,
)

STRIP = 16
LANES = 128
UNROLL = 4


def green(k, xt, yt, zt, zt4, et, xs, ys, zs, area, sj, cj):
    dx = xt - xs
    dy = yt - ys
    planar = dx * dx + dy * dy
    dz = zt - zs
    near = planar + dz * dz + area
    direct = lax.rsqrt(near)
    mirror = lax.rsqrt(near + zt4 * zs)
    kr = k * (planar * lax.rsqrt(jnp.maximum(planar, 1e-30)))
    amp = (et * cj) * lax.rsqrt(1.0 + kr)
    phase = kr + quarter_turn
    n = jnp.floor(phase * inverse_pi + 0.5)
    r = (phase - n * 3.140625) - n * 0.0009676535846665502
    z = r * r
    sin = r + r * (z * (SIN_A[0] + z * (SIN_A[1] + z * (SIN_A[2] + z * SIN_A[3]))))
    cos = 1.0 + z * (COS_B[0] + z * (COS_B[1] + z * (COS_B[2] + z * (COS_B[3] + z * COS_B[4]))))
    amp = jnp.where((n.astype(jnp.int32) & 1) == 1, -amp, amp)
    return sj * (direct + mirror) - amp * sin, amp * cos


def tile_into(k, tb_ref, sb_ref, g, p, tr_ref, ti_ref):
    width = tr_ref.shape[0]
    halves = tr_ref.shape[1] // LANES

    def strip(r, carry):
        rows = pl.ds(pl.multiple_of(r * STRIP, STRIP), STRIP)
        xs = sb_ref[p, 0, rows, :]
        ys = sb_ref[p, 1, rows, :]
        zs = sb_ref[p, 2, rows, :]
        area = sb_ref[p, 3, rows, :]
        sj = sb_ref[p, 4, rows, :]
        cj = sb_ref[p, 5, rows, :]
        for h in range(halves):
            lanes = pl.ds(h * LANES, LANES)
            xt = tb_ref[g, 0, :, lanes]
            yt = tb_ref[g, 1, :, lanes]
            zt = tb_ref[g, 2, :, lanes]
            et = tb_ref[g, 3, :, lanes]
            zt4 = tb_ref[g, 4, :, lanes]
            re, im = green(k, xt, yt, zt, zt4, et, xs, ys, zs, area, sj, cj)
            tr_ref[rows, lanes] = re.astype(jnp.bfloat16)
            ti_ref[rows, lanes] = im.astype(jnp.bfloat16)
        return carry

    lax.fori_loop(0, width // STRIP, strip, 0, unroll=UNROLL)


def entry_product(l_ref, p, tile):
    return jnp.dot(l_ref[p], tile, preferred_element_type=jnp.float32)


def product_kernel(w_ref, k_ref, tb_ref, sb_ref, l_ref, acc_ref, tbuf):
    k = k_ref[0]
    slots = sb_ref.shape[0]
    width = tbuf.shape[0] // 2
    acc_ref[...] = jnp.zeros_like(acc_ref)

    def body(e, carry):
        w = w_ref[e]

        @pl.when(w > 0.0)
        def _():
            g = e // slots
            p = e % slots
            tile_into(k, tb_ref, sb_ref, g, p, tbuf.at[pl.ds(0, width)], tbuf.at[pl.ds(width, width)])
            part = entry_product(l_ref, p, tbuf[...])
            acc_ref[g] = acc_ref[g] + w * part

        return carry

    lax.fori_loop(0, w_ref.shape[0], body, 0)


SMEM_SPEC = pl.BlockSpec(memory_space=pltpu.SMEM)
VMEM_SPEC = pl.BlockSpec(memory_space=pltpu.VMEM)


def product(w_list, k, tb, sb, lhs):
    clusters = tb.shape[0]
    targets = tb.shape[3]
    width = sb.shape[2]
    cols = lhs.shape[1]
    elems = clusters * width * targets * PPT
    return pl.pallas_call(
        product_kernel,
        out_shape=jax.ShapeDtypeStruct((clusters, cols, targets), jnp.float32),
        in_specs=[SMEM_SPEC] * 2 + [VMEM_SPEC] * 3,
        out_specs=VMEM_SPEC,
        scratch_shapes=[pltpu.VMEM((2 * width, targets), jnp.bfloat16)],
        cost_estimate=pl.CostEstimate(
            flops=elems * 60 + 4 * elems * cols,
            transcendentals=elems * 4,
            bytes_accessed=elems * 2,
        ),
    )(w_list, k, tb, sb, lhs)


def scatter_sum(x, axis):
    count = lax.axis_size(axis)
    if count == 1:
        return x
    me = lax.axis_index(axis)
    blocks = x.reshape((count, x.shape[0] // count) + x.shape[1:])
    total = lax.dynamic_index_in_dim(blocks, me, 0, keepdims=False)
    for shift in range(1, count):
        send = lax.dynamic_index_in_dim(blocks, (me + shift) % count, 0, keepdims=False)
        perm = [(i, (i + shift) % count) for i in range(count)]
        total = total + lax.ppermute(send, axis, perm=perm)
    return total


def local(charges, geometry, wavenumber, requests, pairs, counts):
    clus_index = lax.axis_index("clus")
    src_index = lax.axis_index("src")
    sub_index = lax.axis_index("sub")
    clus_count = lax.axis_size("clus")
    sub_count = lax.axis_size("sub")
    source_rows = charges.shape[0]
    share_rows = source_rows // sub_count
    targets = geometry.shape[2]
    cpd = charges.shape[1]
    wavenum = wavenumber[0]
    slot_total = clus_count * requests.shape[2]

    def swap_chunks(x, axis):
        by_shift = [lax.dynamic_index_in_dim(x, clus_index, axis, keepdims=False)]
        for shift in range(1, clus_count):
            send = lax.dynamic_index_in_dim(x, (clus_index + shift) % clus_count, axis, False)
            perm = [(i, (i + shift) % clus_count) for i in range(clus_count)]
            by_shift.append(lax.ppermute(send, "clus", perm=perm))
        stacked = jnp.stack(by_shift, axis=axis)
        return jnp.take(stacked, (clus_index - jnp.arange(clus_count)) % clus_count, axis=axis)

    served = swap_chunks(requests[0], 0).reshape(-1)
    served_index = jnp.maximum(served, 0)
    served_mask = (served >= 0).astype(jnp.bfloat16)[None, :, None]

    def fetch(values):
        picked = jnp.take(values, served_index, axis=1) * served_mask
        chunks = picked.reshape(
            (picked.shape[0], clus_count, picked.shape[1] // clus_count) + picked.shape[2:]
        )
        return swap_chunks(chunks, 1).reshape(picked.shape)

    def lhs_of(values):
        blocks = fetch(values)
        half_width = blocks.shape[2] // 2
        swapped = jnp.concatenate([-blocks[..., half_width:], blocks[..., :half_width]], axis=-1)
        return jnp.concatenate(
            [jnp.transpose(blocks, (1, 2, 0)), jnp.transpose(swapped, (1, 2, 0))], axis=2
        )

    target_geo = lax.dynamic_slice_in_dim(geometry, clus_index * cpd, cpd, axis=1)
    base = jnp.concatenate([target_geo[:3], target_geo[2:3], target_geo[2:3]], axis=0)
    row = jnp.arange(5, dtype=jnp.int32)[:, None, None]
    tq = jnp.where(row == 3, jnp.exp(wavenum * base), jnp.where(row == 4, 4.0 * base, base))
    tb = jnp.broadcast_to(
        jnp.transpose(tq, (1, 0, 2))[:, :, None, :], (cpd, tq.shape[0], STRIP, targets)
    )

    base_ids = jnp.arange(clus_count, dtype=jnp.int32)[:, None] * cpd
    source_ids = (base_ids + jnp.maximum(requests[0], 0)).reshape(-1)
    source_full = jnp.take(geometry, source_ids, axis=1)
    source_geo = lax.dynamic_slice_in_dim(source_full, src_index * source_rows, source_rows, axis=2)
    sj = source_geo[3] * inverse_four_pi
    cj = (two_pi * wavenum) * jnp.exp(wavenum * source_geo[2]) * sj
    sq = jnp.stack([source_geo[0], source_geo[1], source_geo[2], source_geo[3], sj, cj], axis=1)
    sb = jnp.broadcast_to(sq[..., None], sq.shape + (LANES,))

    slot_ids = pairs[:, 0, :]
    live = jnp.arange(pairs.shape[2], dtype=jnp.int32)[None, :] < counts[:, 0:1]
    hits = (slot_ids[:, :, None] == jnp.arange(slot_total, dtype=jnp.int32)[None, None, :]) & live[
        :, :, None
    ]
    w_list = jnp.sum(hits.astype(jnp.float32), axis=1).reshape(-1)
    k_arr = wavenumber.astype(jnp.float32).reshape(1)

    src_count = lax.axis_size("src")

    def finish(acc):
        clusters, cols, _ = acc.shape
        rows = targets // (src_count * sub_count)
        split = acc.reshape(clusters, cols, src_count, sub_count, rows)
        ordered = jnp.transpose(split, (3, 2, 4, 0, 1)).reshape(targets, clusters, cols)
        return scatter_sum(scatter_sum(ordered, "sub"), "src")

    first = finish(product(w_list, k_arr, tb, sb, lhs_of(charges)))
    own_rows = lax.dynamic_slice_in_dim(charges, sub_index * share_rows, share_rows, axis=0)
    iterate_share = (own_rows.astype(jnp.float32) - first).astype(jnp.bfloat16)
    iterate = lax.all_gather(iterate_share, "sub", axis=0, tiled=True)
    image = finish(product(w_list, k_arr, tb, sb, lhs_of(iterate)))
    return (iterate, image)


def solution(mesh):
    in_specs = (
        P(("freq", "src"), "clus", None),
        P(),
        P("freq"),
        P(("clus", "sub"), None, None),
        P("clus", "sub", None),
        P("clus", "sub"),
    )
    out_specs = (P(("freq", "src"), "clus", None), P(("freq", "src", "sub"), "clus", None))
    return jax.shard_map(local, mesh=mesh, in_specs=in_specs, out_specs=out_specs, check_vma=False)
```

```python
import jax
import jax.numpy as jnp
from jax import lax
from jax.experimental import pallas as pl
from jax.experimental.pallas import tpu as pltpu
from jax.sharding import PartitionSpec as P

CPD = 12
CAP = 4
PPT = 32

quarter_turn = 0.7853981633974483
two_pi = 6.283185307179586
inverse_four_pi = 0.07957747154594767
inverse_pi = 0.3183098861837907
SIN_A = (-0.16666661577130884, 0.008333118573140752, -0.00019813475437141734, 2.6144256303410747e-06)
COS_B = (
    -0.4999999981796688,
    0.041666651863571776,
    -0.0013888547499597086,
    2.4769209821955003e-05,
    -2.620509973872218e-07,
)

STRIP = 16
LANES = 128
UNROLL = 4


def green(k, xt, yt, zt, zt4, et, xs, ys, zs, area, sj, cj):
    dx = xt - xs
    dy = yt - ys
    planar = dx * dx + dy * dy
    dz = zt - zs
    near = planar + dz * dz + area
    direct = lax.rsqrt(near)
    mirror = lax.rsqrt(near + zt4 * zs)
    kr = k * (planar * lax.rsqrt(jnp.maximum(planar, 1e-30)))
    amp = (et * cj) * lax.rsqrt(1.0 + kr)
    phase = kr + quarter_turn
    n = jnp.floor(phase * inverse_pi + 0.5)
    r = (phase - n * 3.140625) - n * 0.0009676535846665502
    z = r * r
    sin = r + r * (z * (SIN_A[0] + z * (SIN_A[1] + z * (SIN_A[2] + z * SIN_A[3]))))
    cos = 1.0 + z * (COS_B[0] + z * (COS_B[1] + z * (COS_B[2] + z * (COS_B[3] + z * COS_B[4]))))
    amp = jnp.where((n.astype(jnp.int32) & 1) == 1, -amp, amp)
    return sj * (direct + mirror) - amp * sin, amp * cos


def tile_into(k, tb_ref, sb_ref, g, p, tr_ref, ti_ref):
    width = tr_ref.shape[0]
    halves = tr_ref.shape[1] // LANES

    def strip(r, carry):
        rows = pl.ds(pl.multiple_of(r * STRIP, STRIP), STRIP)
        xs = sb_ref[p, 0, rows, :]
        ys = sb_ref[p, 1, rows, :]
        zs = sb_ref[p, 2, rows, :]
        area = sb_ref[p, 3, rows, :]
        sj = sb_ref[p, 4, rows, :]
        cj = sb_ref[p, 5, rows, :]
        for h in range(halves):
            lanes = pl.ds(h * LANES, LANES)
            xt = tb_ref[g, 0, :, lanes]
            yt = tb_ref[g, 1, :, lanes]
            zt = tb_ref[g, 2, :, lanes]
            et = tb_ref[g, 3, :, lanes]
            zt4 = tb_ref[g, 4, :, lanes]
            re, im = green(k, xt, yt, zt, zt4, et, xs, ys, zs, area, sj, cj)
            tr_ref[rows, lanes] = re.astype(jnp.bfloat16)
            ti_ref[rows, lanes] = im.astype(jnp.bfloat16)
        return carry

    lax.fori_loop(0, width // STRIP, strip, 0, unroll=UNROLL)


def entry_product(l_ref, p, tile):
    return jnp.dot(l_ref[p], tile, preferred_element_type=jnp.float32)


def product_kernel(w_ref, k_ref, tb_ref, sb_ref, l_ref, acc_ref, tbuf):
    k = k_ref[0]
    slots = sb_ref.shape[0]
    width = tbuf.shape[0] // 2
    acc_ref[...] = jnp.zeros_like(acc_ref)

    def body(e, carry):
        w = w_ref[e]

        @pl.when(w > 0.0)
        def _():
            g = e // slots
            p = e % slots
            tile_into(k, tb_ref, sb_ref, g, p, tbuf.at[pl.ds(0, width)], tbuf.at[pl.ds(width, width)])
            part = entry_product(l_ref, p, tbuf[...])
            acc_ref[g] = acc_ref[g] + w * part

        return carry

    lax.fori_loop(0, w_ref.shape[0], body, 0)


SMEM_SPEC = pl.BlockSpec(memory_space=pltpu.SMEM)
VMEM_SPEC = pl.BlockSpec(memory_space=pltpu.VMEM)


def product(w_list, k, tb, sb, lhs):
    clusters = tb.shape[0]
    targets = tb.shape[3]
    width = sb.shape[2]
    cols = lhs.shape[1]
    elems = clusters * width * targets * PPT
    return pl.pallas_call(
        product_kernel,
        out_shape=jax.ShapeDtypeStruct((clusters, cols, targets), jnp.float32),
        in_specs=[SMEM_SPEC] * 2 + [VMEM_SPEC] * 3,
        out_specs=VMEM_SPEC,
        scratch_shapes=[pltpu.VMEM((2 * width, targets), jnp.bfloat16)],
        cost_estimate=pl.CostEstimate(
            flops=elems * 60 + 4 * elems * cols,
            transcendentals=elems * 4,
            bytes_accessed=elems * 2,
        ),
    )(w_list, k, tb, sb, lhs)


def scatter_sum(x, axis):
    count = lax.axis_size(axis)
    if count == 1:
        return x
    me = lax.axis_index(axis)
    blocks = x.reshape((count, x.shape[0] // count) + x.shape[1:])
    total = lax.dynamic_index_in_dim(blocks, me, 0, keepdims=False)
    for shift in range(1, count):
        send = lax.dynamic_index_in_dim(blocks, (me + shift) % count, 0, keepdims=False)
        perm = [(i, (i + shift) % count) for i in range(count)]
        total = total + lax.ppermute(send, axis, perm=perm)
    return total


def local(charges, geometry, wavenumber, requests, pairs, counts):
    clus_index = lax.axis_index("clus")
    src_index = lax.axis_index("src")
    sub_index = lax.axis_index("sub")
    clus_count = lax.axis_size("clus")
    sub_count = lax.axis_size("sub")
    source_rows = charges.shape[0]
    share_rows = source_rows // sub_count
    targets = geometry.shape[2]
    cpd = charges.shape[1]
    wavenum = wavenumber[0]
    slot_total = clus_count * requests.shape[2]

    def swap_chunks(x, axis):
        by_shift = [lax.dynamic_index_in_dim(x, clus_index, axis, keepdims=False)]
        for shift in range(1, clus_count):
            send = lax.dynamic_index_in_dim(x, (clus_index + shift) % clus_count, axis, False)
            perm = [(i, (i + shift) % clus_count) for i in range(clus_count)]
            by_shift.append(lax.ppermute(send, "clus", perm=perm))
        stacked = jnp.stack(by_shift, axis=axis)
        return jnp.take(stacked, (clus_index - jnp.arange(clus_count)) % clus_count, axis=axis)

    served = swap_chunks(requests[0], 0).reshape(-1)
    served_index = jnp.maximum(served, 0)
    served_mask = (served >= 0).astype(jnp.bfloat16)[None, :, None]

    def fetch(values):
        picked = jnp.take(values, served_index, axis=1) * served_mask
        chunks = picked.reshape(
            (picked.shape[0], clus_count, picked.shape[1] // clus_count) + picked.shape[2:]
        )
        return swap_chunks(chunks, 1).reshape(picked.shape)

    def lhs_of(values):
        blocks = fetch(values)
        half_width = blocks.shape[2] // 2
        swapped = jnp.concatenate([-blocks[..., half_width:], blocks[..., :half_width]], axis=-1)
        return jnp.concatenate(
            [jnp.transpose(blocks, (1, 2, 0)), jnp.transpose(swapped, (1, 2, 0))], axis=2
        )

    target_geo = lax.dynamic_slice_in_dim(geometry, clus_index * cpd, cpd, axis=1)
    base = jnp.concatenate([target_geo[:3], target_geo[2:3], target_geo[2:3]], axis=0)
    row = jnp.arange(5, dtype=jnp.int32)[:, None, None]
    tq = jnp.where(row == 3, jnp.exp(wavenum * base), jnp.where(row == 4, 4.0 * base, base))
    tb = jnp.broadcast_to(
        jnp.transpose(tq, (1, 0, 2))[:, :, None, :], (cpd, tq.shape[0], STRIP, targets)
    )

    base_ids = jnp.arange(clus_count, dtype=jnp.int32)[:, None] * cpd
    source_ids = (base_ids + jnp.maximum(requests[0], 0)).reshape(-1)
    source_full = jnp.take(geometry, source_ids, axis=1)
    source_geo = lax.dynamic_slice_in_dim(source_full, src_index * source_rows, source_rows, axis=2)
    sj = source_geo[3] * inverse_four_pi
    cj = (two_pi * wavenum) * jnp.exp(wavenum * source_geo[2]) * sj
    sq = jnp.stack([source_geo[0], source_geo[1], source_geo[2], source_geo[3], sj, cj], axis=1)
    sb = jnp.broadcast_to(sq[..., None], sq.shape + (LANES,))

    slot_ids = pairs[:, 0, :]
    live = jnp.arange(pairs.shape[2], dtype=jnp.int32)[None, :] < counts[:, 0:1]
    hits = (slot_ids[:, :, None] == jnp.arange(slot_total, dtype=jnp.int32)[None, None, :]) & live[
        :, :, None
    ]
    w_list = jnp.sum(hits.astype(jnp.float32), axis=1).reshape(-1)
    k_arr = wavenumber.astype(jnp.float32).reshape(1)

    src_count = lax.axis_size("src")

    def finish(acc):
        clusters, cols, _ = acc.shape
        rows = targets // (src_count * sub_count)
        split = acc.reshape(clusters, cols, src_count, sub_count, rows)
        ordered = jnp.transpose(split, (3, 2, 4, 0, 1)).reshape(targets, clusters, cols)
        return scatter_sum(scatter_sum(ordered, "sub"), "src")

    def split_product(lhs):
        cut = cpd // 2
        parts = []
        for lo, hi in ((0, cut), (cut, cpd)):
            w_part = w_list[lo * slot_total : hi * slot_total]
            parts.append(finish(product(w_part, k_arr, tb[lo:hi], sb, lhs)))
        return jnp.concatenate(parts, axis=1)

    first = split_product(lhs_of(charges))
    own_rows = lax.dynamic_slice_in_dim(charges, sub_index * share_rows, share_rows, axis=0)
    iterate_share = (own_rows.astype(jnp.float32) - first).astype(jnp.bfloat16)
    iterate = lax.all_gather(iterate_share, "sub", axis=0, tiled=True)
    image = split_product(lhs_of(iterate))
    return (iterate, image)


def solution(mesh):
    in_specs = (
        P(("freq", "src"), "clus", None),
        P(),
        P("freq"),
        P(("clus", "sub"), None, None),
        P("clus", "sub", None),
        P("clus", "sub"),
    )
    out_specs = (P(("freq", "src"), "clus", None), P(("freq", "src", "sub"), "clus", None))
    return jax.shard_map(local, mesh=mesh, in_specs=in_specs, out_specs=out_specs, check_vma=False)
```

```python
import jax
import jax.numpy as jnp
from jax import lax
from jax.experimental import pallas as pl
from jax.experimental.pallas import tpu as pltpu
from jax.sharding import PartitionSpec as P

CPD = 12
CAP = 4
PPT = 32

quarter_turn = 0.7853981633974483
two_pi = 6.283185307179586
inverse_four_pi = 0.07957747154594767
inverse_pi = 0.3183098861837907
SIN_A = (-0.16666661577130884, 0.008333118573140752, -0.00019813475437141734, 2.6144256303410747e-06)
COS_B = (
    -0.4999999981796688,
    0.041666651863571776,
    -0.0013888547499597086,
    2.4769209821955003e-05,
    -2.620509973872218e-07,
)

STRIP = 16
LANES = 128


def green(k, xt, yt, zt, zt4, et, xs, ys, zs, area, sj, cj):
    dx = xt - xs
    dy = yt - ys
    planar = dx * dx + dy * dy
    dz = zt - zs
    near = planar + dz * dz + area
    direct = lax.rsqrt(near)
    mirror = lax.rsqrt(near + zt4 * zs)
    kr = k * (planar * lax.rsqrt(jnp.maximum(planar, 1e-30)))
    amp = (et * cj) * lax.rsqrt(1.0 + kr)
    phase = kr + quarter_turn
    n = jnp.floor(phase * inverse_pi + 0.5)
    r = (phase - n * 3.140625) - n * 0.0009676535846665502
    z = r * r
    sin = r + r * (z * (SIN_A[0] + z * (SIN_A[1] + z * (SIN_A[2] + z * SIN_A[3]))))
    cos = 1.0 + z * (COS_B[0] + z * (COS_B[1] + z * (COS_B[2] + z * (COS_B[3] + z * COS_B[4]))))
    amp = jnp.where((n.astype(jnp.int32) & 1) == 1, -amp, amp)
    return sj * (direct + mirror) - amp * sin, amp * cos


def tile_into(k, tb_ref, sb_ref, g, p, tr_ref, ti_ref):
    width = tr_ref.shape[0]
    halves = tr_ref.shape[1] // LANES

    def strip(r, carry):
        rows = pl.ds(pl.multiple_of(r * STRIP, STRIP), STRIP)
        xs = sb_ref[p, 0, rows, :]
        ys = sb_ref[p, 1, rows, :]
        zs = sb_ref[p, 2, rows, :]
        area = sb_ref[p, 3, rows, :]
        sj = sb_ref[p, 4, rows, :]
        cj = sb_ref[p, 5, rows, :]
        for h in range(halves):
            lanes = pl.ds(h * LANES, LANES)
            xt = tb_ref[g, 0, :, lanes]
            yt = tb_ref[g, 1, :, lanes]
            zt = tb_ref[g, 2, :, lanes]
            et = tb_ref[g, 3, :, lanes]
            zt4 = tb_ref[g, 4, :, lanes]
            re, im = green(k, xt, yt, zt, zt4, et, xs, ys, zs, area, sj, cj)
            tr_ref[rows, lanes] = re.astype(jnp.bfloat16)
            ti_ref[rows, lanes] = im.astype(jnp.bfloat16)
        return carry

    for r in range(width // STRIP):
        strip(r, 0)


def entry_product(l_ref, p, tile):
    return jnp.dot(l_ref[p], tile, preferred_element_type=jnp.float32)


def product_kernel(w_ref, k_ref, tb_ref, sb_ref, l_ref, acc_ref, tbuf, idx_ref):
    k = k_ref[0]
    slots = sb_ref.shape[0]
    width = tbuf.shape[1] // 2
    acc_ref[...] = jnp.zeros_like(acc_ref)

    def gather(e, n):
        idx_ref[n] = e
        return n + (w_ref[e] > 0.0).astype(jnp.int32)

    n = lax.fori_loop(0, w_ref.shape[0], gather, 0)

    def build(e, slot):
        tile_into(k, tb_ref, sb_ref, e // slots, e % slots, tbuf.at[slot, pl.ds(0, width)],
                  tbuf.at[slot, pl.ds(width, width)])

    @pl.when(n > 0)
    def _():
        build(idx_ref[0], 0)

        def body(i, carry):
            e = idx_ref[i]
            nxt = idx_ref[jnp.minimum(i + 1, n - 1)]
            slot = i % 2
            build(nxt, 1 - slot)
            g = e // slots
            part = entry_product(l_ref, e % slots, tbuf[slot])
            acc_ref[g] = acc_ref[g] + w_ref[e] * part
            return carry

        lax.fori_loop(0, n, body, 0)


SMEM_SPEC = pl.BlockSpec(memory_space=pltpu.SMEM)
VMEM_SPEC = pl.BlockSpec(memory_space=pltpu.VMEM)


def product(w_list, k, tb, sb, lhs):
    clusters = tb.shape[0]
    targets = tb.shape[3]
    width = sb.shape[2]
    cols = lhs.shape[1]
    elems = clusters * width * targets * PPT
    return pl.pallas_call(
        product_kernel,
        out_shape=jax.ShapeDtypeStruct((clusters, cols, targets), jnp.float32),
        in_specs=[SMEM_SPEC] * 2 + [VMEM_SPEC] * 3,
        out_specs=VMEM_SPEC,
        scratch_shapes=[
            pltpu.VMEM((2, 2 * width, targets), jnp.bfloat16),
            pltpu.SMEM((w_list.shape[0],), jnp.int32),
        ],
        cost_estimate=pl.CostEstimate(
            flops=elems * 60 + 4 * elems * cols,
            transcendentals=elems * 4,
            bytes_accessed=elems * 2,
        ),
    )(w_list, k, tb, sb, lhs)


def scatter_sum(x, axis):
    count = lax.axis_size(axis)
    if count == 1:
        return x
    me = lax.axis_index(axis)
    blocks = x.reshape((count, x.shape[0] // count) + x.shape[1:])
    total = lax.dynamic_index_in_dim(blocks, me, 0, keepdims=False)
    for shift in range(1, count):
        send = lax.dynamic_index_in_dim(blocks, (me + shift) % count, 0, keepdims=False)
        perm = [(i, (i + shift) % count) for i in range(count)]
        total = total + lax.ppermute(send, axis, perm=perm)
    return total


def local(charges, geometry, wavenumber, requests, pairs, counts):
    clus_index = lax.axis_index("clus")
    src_index = lax.axis_index("src")
    sub_index = lax.axis_index("sub")
    clus_count = lax.axis_size("clus")
    sub_count = lax.axis_size("sub")
    source_rows = charges.shape[0]
    share_rows = source_rows // sub_count
    targets = geometry.shape[2]
    cpd = charges.shape[1]
    wavenum = wavenumber[0]
    slot_total = clus_count * requests.shape[2]

    def swap_chunks(x, axis):
        by_shift = [lax.dynamic_index_in_dim(x, clus_index, axis, keepdims=False)]
        for shift in range(1, clus_count):
            send = lax.dynamic_index_in_dim(x, (clus_index + shift) % clus_count, axis, False)
            perm = [(i, (i + shift) % clus_count) for i in range(clus_count)]
            by_shift.append(lax.ppermute(send, "clus", perm=perm))
        stacked = jnp.stack(by_shift, axis=axis)
        return jnp.take(stacked, (clus_index - jnp.arange(clus_count)) % clus_count, axis=axis)

    served = swap_chunks(requests[0], 0).reshape(-1)
    served_index = jnp.maximum(served, 0)
    served_mask = (served >= 0).astype(jnp.bfloat16)[None, :, None]

    def fetch(values):
        picked = jnp.take(values, served_index, axis=1) * served_mask
        chunks = picked.reshape(
            (picked.shape[0], clus_count, picked.shape[1] // clus_count) + picked.shape[2:]
        )
        return swap_chunks(chunks, 1).reshape(picked.shape)

    def lhs_of(values):
        blocks = fetch(values)
        half_width = blocks.shape[2] // 2
        swapped = jnp.concatenate([-blocks[..., half_width:], blocks[..., :half_width]], axis=-1)
        return jnp.concatenate(
            [jnp.transpose(blocks, (1, 2, 0)), jnp.transpose(swapped, (1, 2, 0))], axis=2
        )

    target_geo = lax.dynamic_slice_in_dim(geometry, clus_index * cpd, cpd, axis=1)
    base = jnp.concatenate([target_geo[:3], target_geo[2:3], target_geo[2:3]], axis=0)
    row = jnp.arange(5, dtype=jnp.int32)[:, None, None]
    tq = jnp.where(row == 3, jnp.exp(wavenum * base), jnp.where(row == 4, 4.0 * base, base))
    tb = jnp.broadcast_to(
        jnp.transpose(tq, (1, 0, 2))[:, :, None, :], (cpd, tq.shape[0], STRIP, targets)
    )

    base_ids = jnp.arange(clus_count, dtype=jnp.int32)[:, None] * cpd
    source_ids = (base_ids + jnp.maximum(requests[0], 0)).reshape(-1)
    source_full = jnp.take(geometry, source_ids, axis=1)
    source_geo = lax.dynamic_slice_in_dim(source_full, src_index * source_rows, source_rows, axis=2)
    sj = source_geo[3] * inverse_four_pi
    cj = (two_pi * wavenum) * jnp.exp(wavenum * source_geo[2]) * sj
    sq = jnp.stack([source_geo[0], source_geo[1], source_geo[2], source_geo[3], sj, cj], axis=1)
    sb = jnp.broadcast_to(sq[..., None], sq.shape + (LANES,))

    slot_ids = pairs[:, 0, :]
    live = jnp.arange(pairs.shape[2], dtype=jnp.int32)[None, :] < counts[:, 0:1]
    hits = (slot_ids[:, :, None] == jnp.arange(slot_total, dtype=jnp.int32)[None, None, :]) & live[
        :, :, None
    ]
    w_list = jnp.sum(hits.astype(jnp.float32), axis=1).reshape(-1)
    k_arr = wavenumber.astype(jnp.float32).reshape(1)

    src_count = lax.axis_size("src")

    def finish(acc):
        clusters, cols, _ = acc.shape
        rows = targets // (src_count * sub_count)
        split = acc.reshape(clusters, cols, src_count, sub_count, rows)
        ordered = jnp.transpose(split, (3, 2, 4, 0, 1)).reshape(targets, clusters, cols)
        return scatter_sum(scatter_sum(ordered, "sub"), "src")

    first = finish(product(w_list, k_arr, tb, sb, lhs_of(charges)))
    own_rows = lax.dynamic_slice_in_dim(charges, sub_index * share_rows, share_rows, axis=0)
    iterate_share = (own_rows.astype(jnp.float32) - first).astype(jnp.bfloat16)
    iterate = lax.all_gather(iterate_share, "sub", axis=0, tiled=True)
    image = finish(product(w_list, k_arr, tb, sb, lhs_of(iterate)))
    return (iterate, image)


def solution(mesh):
    in_specs = (
        P(("freq", "src"), "clus", None),
        P(),
        P("freq"),
        P(("clus", "sub"), None, None),
        P("clus", "sub", None),
        P("clus", "sub"),
    )
    out_specs = (P(("freq", "src"), "clus", None), P(("freq", "src", "sub"), "clus", None))
    return jax.shard_map(local, mesh=mesh, in_specs=in_specs, out_specs=out_specs, check_vma=False)
```

```python
import jax
import jax.numpy as jnp
from jax import lax
from jax.experimental import pallas as pl
from jax.experimental.pallas import tpu as pltpu
from jax.sharding import PartitionSpec as P

CPD = 12
CAP = 4
PPT = 32

quarter_turn = 0.7853981633974483
two_pi = 6.283185307179586
inverse_four_pi = 0.07957747154594767
inverse_pi = 0.3183098861837907
SIN_A = (-0.16666661577130884, 0.008333118573140752, -0.00019813475437141734, 2.6144256303410747e-06)
COS_B = (
    -0.4999999981796688,
    0.041666651863571776,
    -0.0013888547499597086,
    2.4769209821955003e-05,
    -2.620509973872218e-07,
)

STRIP = 16
LANES = 128


def green(k, xt, yt, zt, zt4, et, xs, ys, zs, area, sj, cj):
    dx = xt - xs
    dy = yt - ys
    planar = dx * dx + dy * dy
    dz = zt - zs
    near = planar + dz * dz + area
    direct = lax.rsqrt(near)
    mirror = lax.rsqrt(near + zt4 * zs)
    kr = k * (planar * lax.rsqrt(jnp.maximum(planar, 1e-30)))
    amp = (et * cj) * lax.rsqrt(1.0 + kr)
    phase = kr + quarter_turn
    n = jnp.floor(phase * inverse_pi + 0.5)
    r = (phase - n * 3.140625) - n * 0.0009676535846665502
    z = r * r
    sin = r + r * (z * (SIN_A[0] + z * (SIN_A[1] + z * (SIN_A[2] + z * SIN_A[3]))))
    cos = 1.0 + z * (COS_B[0] + z * (COS_B[1] + z * (COS_B[2] + z * (COS_B[3] + z * COS_B[4]))))
    amp = jnp.where((n.astype(jnp.int32) & 1) == 1, -amp, amp)
    return sj * (direct + mirror) - amp * sin, amp * cos


def tile_into(k, tb_ref, sb_ref, g, p, tr_ref, ti_ref):
    width = tr_ref.shape[0]
    halves = tr_ref.shape[1] // LANES

    def strip(r, carry):
        rows = pl.ds(pl.multiple_of(r * STRIP, STRIP), STRIP)
        xs = sb_ref[p, 0, rows, :]
        ys = sb_ref[p, 1, rows, :]
        zs = sb_ref[p, 2, rows, :]
        area = sb_ref[p, 3, rows, :]
        sj = sb_ref[p, 4, rows, :]
        cj = sb_ref[p, 5, rows, :]
        for h in range(halves):
            lanes = pl.ds(h * LANES, LANES)
            xt = tb_ref[g, 0, :, lanes]
            yt = tb_ref[g, 1, :, lanes]
            zt = tb_ref[g, 2, :, lanes]
            et = tb_ref[g, 3, :, lanes]
            zt4 = tb_ref[g, 4, :, lanes]
            re, im = green(k, xt, yt, zt, zt4, et, xs, ys, zs, area, sj, cj)
            tr_ref[rows, lanes] = re.astype(jnp.bfloat16)
            ti_ref[rows, lanes] = im.astype(jnp.bfloat16)
        return carry

    for r in range(width // STRIP):
        strip(r, 0)


def entry_product(l_ref, p, tile):
    return jnp.dot(l_ref[p], tile, preferred_element_type=jnp.float32)


def product_kernel(w_ref, k_ref, tb_ref, sb_ref, l_ref, acc_ref, tbuf, idx_ref):
    k = k_ref[0]
    slots = sb_ref.shape[0]
    width = tbuf.shape[1] // 2
    acc_ref[...] = jnp.zeros_like(acc_ref)

    def gather(e, n):
        idx_ref[n] = e
        return n + (w_ref[e] > 0.0).astype(jnp.int32)

    n = lax.fori_loop(0, w_ref.shape[0], gather, 0, unroll=8)

    def build(e, slot):
        tile_into(k, tb_ref, sb_ref, e // slots, e % slots, tbuf.at[slot, pl.ds(0, width)],
                  tbuf.at[slot, pl.ds(width, width)])

    @pl.when(n > 0)
    def _():
        build(idx_ref[0], 0)

        def body(i, carry):
            e = idx_ref[i]
            nxt = idx_ref[jnp.minimum(i + 1, n - 1)]
            slot = i % 2
            build(nxt, 1 - slot)
            g = e // slots
            part = entry_product(l_ref, e % slots, tbuf[slot])
            acc_ref[g] = acc_ref[g] + w_ref[e] * part
            return carry

        lax.fori_loop(0, n, body, 0)


SMEM_SPEC = pl.BlockSpec(memory_space=pltpu.SMEM)
VMEM_SPEC = pl.BlockSpec(memory_space=pltpu.VMEM)


def product(w_list, k, tb, sb, lhs):
    clusters = tb.shape[0]
    targets = tb.shape[3]
    width = sb.shape[2]
    cols = lhs.shape[1]
    elems = clusters * width * targets * PPT
    return pl.pallas_call(
        product_kernel,
        out_shape=jax.ShapeDtypeStruct((clusters, cols, targets), jnp.float32),
        in_specs=[SMEM_SPEC] * 2 + [VMEM_SPEC] * 3,
        out_specs=VMEM_SPEC,
        scratch_shapes=[
            pltpu.VMEM((2, 2 * width, targets), jnp.bfloat16),
            pltpu.SMEM((w_list.shape[0],), jnp.int32),
        ],
        cost_estimate=pl.CostEstimate(
            flops=elems * 60 + 4 * elems * cols,
            transcendentals=elems * 4,
            bytes_accessed=elems * 2,
        ),
    )(w_list, k, tb, sb, lhs)


def scatter_sum(x, axis):
    count = lax.axis_size(axis)
    if count == 1:
        return x
    me = lax.axis_index(axis)
    blocks = x.reshape((count, x.shape[0] // count) + x.shape[1:])
    total = lax.dynamic_index_in_dim(blocks, me, 0, keepdims=False)
    for shift in range(1, count):
        send = lax.dynamic_index_in_dim(blocks, (me + shift) % count, 0, keepdims=False)
        perm = [(i, (i + shift) % count) for i in range(count)]
        total = total + lax.ppermute(send, axis, perm=perm)
    return total


def local(charges, geometry, wavenumber, requests, pairs, counts):
    clus_index = lax.axis_index("clus")
    src_index = lax.axis_index("src")
    sub_index = lax.axis_index("sub")
    clus_count = lax.axis_size("clus")
    sub_count = lax.axis_size("sub")
    source_rows = charges.shape[0]
    share_rows = source_rows // sub_count
    targets = geometry.shape[2]
    cpd = charges.shape[1]
    wavenum = wavenumber[0]
    slot_total = clus_count * requests.shape[2]

    def swap_chunks(x, axis):
        by_shift = [lax.dynamic_index_in_dim(x, clus_index, axis, keepdims=False)]
        for shift in range(1, clus_count):
            send = lax.dynamic_index_in_dim(x, (clus_index + shift) % clus_count, axis, False)
            perm = [(i, (i + shift) % clus_count) for i in range(clus_count)]
            by_shift.append(lax.ppermute(send, "clus", perm=perm))
        stacked = jnp.stack(by_shift, axis=axis)
        return jnp.take(stacked, (clus_index - jnp.arange(clus_count)) % clus_count, axis=axis)

    served = swap_chunks(requests[0], 0).reshape(-1)
    served_index = jnp.maximum(served, 0)
    served_mask = (served >= 0).astype(jnp.bfloat16)[None, :, None]

    def fetch(values):
        picked = jnp.take(values, served_index, axis=1) * served_mask
        chunks = picked.reshape(
            (picked.shape[0], clus_count, picked.shape[1] // clus_count) + picked.shape[2:]
        )
        return swap_chunks(chunks, 1).reshape(picked.shape)

    def lhs_of(values):
        blocks = fetch(values)
        half_width = blocks.shape[2] // 2
        swapped = jnp.concatenate([-blocks[..., half_width:], blocks[..., :half_width]], axis=-1)
        return jnp.concatenate(
            [jnp.transpose(blocks, (1, 2, 0)), jnp.transpose(swapped, (1, 2, 0))], axis=2
        )

    target_geo = lax.dynamic_slice_in_dim(geometry, clus_index * cpd, cpd, axis=1)
    base = jnp.concatenate([target_geo[:3], target_geo[2:3], target_geo[2:3]], axis=0)
    row = jnp.arange(5, dtype=jnp.int32)[:, None, None]
    tq = jnp.where(row == 3, jnp.exp(wavenum * base), jnp.where(row == 4, 4.0 * base, base))
    tb = jnp.broadcast_to(
        jnp.transpose(tq, (1, 0, 2))[:, :, None, :], (cpd, tq.shape[0], STRIP, targets)
    )

    base_ids = jnp.arange(clus_count, dtype=jnp.int32)[:, None] * cpd
    source_ids = (base_ids + jnp.maximum(requests[0], 0)).reshape(-1)
    source_full = jnp.take(geometry, source_ids, axis=1)
    source_geo = lax.dynamic_slice_in_dim(source_full, src_index * source_rows, source_rows, axis=2)
    sj = source_geo[3] * inverse_four_pi
    cj = (two_pi * wavenum) * jnp.exp(wavenum * source_geo[2]) * sj
    sq = jnp.stack([source_geo[0], source_geo[1], source_geo[2], source_geo[3], sj, cj], axis=1)
    sb = jnp.broadcast_to(sq[..., None], sq.shape + (LANES,))

    slot_ids = pairs[:, 0, :]
    live = jnp.arange(pairs.shape[2], dtype=jnp.int32)[None, :] < counts[:, 0:1]
    hits = (slot_ids[:, :, None] == jnp.arange(slot_total, dtype=jnp.int32)[None, None, :]) & live[
        :, :, None
    ]
    w_list = jnp.sum(hits.astype(jnp.float32), axis=1).reshape(-1)
    k_arr = wavenumber.astype(jnp.float32).reshape(1)

    src_count = lax.axis_size("src")

    def finish(acc):
        clusters, cols, _ = acc.shape
        rows = targets // (src_count * sub_count)
        split = acc.reshape(clusters, cols, src_count, sub_count, rows)
        ordered = jnp.transpose(split, (3, 2, 4, 0, 1)).reshape(targets, clusters, cols)
        return scatter_sum(scatter_sum(ordered, "sub"), "src")

    first = finish(product(w_list, k_arr, tb, sb, lhs_of(charges)))
    own_rows = lax.dynamic_slice_in_dim(charges, sub_index * share_rows, share_rows, axis=0)
    iterate_share = (own_rows.astype(jnp.float32) - first).astype(jnp.bfloat16)
    iterate = lax.all_gather(iterate_share, "sub", axis=0, tiled=True)
    image = finish(product(w_list, k_arr, tb, sb, lhs_of(iterate)))
    return (iterate, image)


def solution(mesh):
    in_specs = (
        P(("freq", "src"), "clus", None),
        P(),
        P("freq"),
        P(("clus", "sub"), None, None),
        P("clus", "sub", None),
        P("clus", "sub"),
    )
    out_specs = (P(("freq", "src"), "clus", None), P(("freq", "src", "sub"), "clus", None))
    return jax.shard_map(local, mesh=mesh, in_specs=in_specs, out_specs=out_specs, check_vma=False)
```
